256 devices in a mesh: dp: 16 (over x, y), tensor: 16 (over z, core).
Axes of the slice: x: 4, y: 4, z: 8, core: 2. Of those that a mesh axis runs over, the one named last changes fastest.
Arguments:
- tokens: bfloat16 [2048, 8192], P('tensor', 'dp'), may hold values from -6 to 6
- cotangent: bfloat16 [2048, 8192], P('tensor', 'dp'), may hold values from -0.625 to 0.625
- gate_weight: bfloat16 [8192, 14336], P('dp', 'tensor'), may hold values from -0.0625 to 0.0625
- up_weight: bfloat16 [8192, 14336], P('dp', 'tensor'), may hold values from -0.0625 to 0.0625
- down_weight: bfloat16 [14336, 8192], P('tensor', 'dp'), may hold values from -0.046875 to 0.046875
- gate_in: bfloat16 [64, 8192, 16], P(None, 'dp'), may hold values from -0.0625 to 0.0625
- up_in: bfloat16 [64, 8192, 16], P(None, 'dp'), may hold values from -0.0625 to 0.0625
- down_out: bfloat16 [64, 16, 8192], P(None, None, 'dp'), may hold values from -1.5 to 1.5
- gate_out: bfloat16 [64, 16, 14336], P(None, None, 'tensor'), may hold values from -1.5 to 1.5
- up_out: bfloat16 [64, 16, 14336], P(None, None, 'tensor'), may hold values from -1.5 to 1.5
- down_in: bfloat16 [64, 14336, 16], P(None, 'tensor'), may hold values from -0.046875 to 0.046875
- tenants: int32 [32], replicated, may hold values from 0 to 63
- owners: int32 [64], replicated, may hold values from 0 to 63, each once
Outputs:
- mixed: bfloat16 [2048, 8192], P('tensor', 'dp')
- grad_gate_in: float32 [64, 8192, 16], P('tensor', 'dp')
- grad_up_in: float32 [64, 8192, 16], P('tensor', 'dp')
- grad_down_out: float32 [64, 16, 8192], P('tensor', None, 'dp')
- grad_gate_out: float32 [64, 16, 14336], P('dp', None, 'tensor')
- grad_up_out: float32 [64, 16, 14336], P('dp', None, 'tensor')
- grad_down_in: float32 [64, 14336, 16], P('dp', 'tensor')
The draws below stay inside these ranges and needn't reach their ends.
Inputs may be any that keep to these rules, and one draw needn't show every extreme that they name: `tenants`: tenant numbers lie in 0 to 63; a tenant may own no block. `owners`: every owner slot is given to exactly one tenant.
All inputs are finite; a program needn't handle non-finite values.
Results may differ from the reference program's by a relative error of at most 0.029.
Values may be sent and summed in bfloat16 or wider, within the bound.
No kernel may reach another device: no remote copies, remote signals or barrier semaphores. Data moves between devices by JAX's collectives and lax.ppermute only.
A program may use at most 128 MiB of HBM per device.

```python
import math
import jax
import jax.numpy as jnp
import numpy as np
from jax import lax

MODEL_WIDTH = 8192
FFW = 14336
R = 16
BLOCK = 64
TENANTS = 64
TOKENS = 2048
NBLK = 32
N_DP = 16
N_TENSOR = 16


def set_ends(result, own_key, least, high):
    extent = result.shape
    place = [jax.random.randint(jax.random.fold_in(own_key, axis), (), 0, extent[axis]) for axis in range(len(extent))]
    result = result.at[tuple(place)].set(least)
    longest = extent.index(max(extent))
    place[longest] = (place[longest] + 1) % extent[longest]
    return result.at[tuple(place)].set(high)


def block_levels(own_key, shape, cuts, smallest, high):
    level = 1.0
    for axis_at, shards_of in cuts:
        draws = jax.random.uniform(jax.random.fold_in(jax.random.fold_in(own_key, 6), axis_at), (shards_of,), jnp.float32, smallest / len(cuts), high / len(cuts))
        level = level * jnp.repeat(jnp.exp(draws), shape[axis_at] // shards_of).reshape((-1,) + (1,) * (len(shape) - 1 - axis_at))
    return level


def rank_bounds(amount, slope):
    portions = [(1 << 20) // math.isqrt(rank ** slope) + 1 for rank in range(1, amount + 1)]
    scale = 1 + sum(portions) // (1 << 30)
    return np.cumsum(np.array([max(1, weight // scale) for weight in portions]))


def ranked(stream_key, dims, number_of, lean):
    listing = rank_bounds(number_of, lean)
    lot = jax.random.randint(jax.random.fold_in(stream_key, 1), dims, 0, int(listing[number_of - 1]))
    grade = jnp.searchsorted(jnp.asarray(listing, jnp.int32), lot, side="right")
    return jax.random.permutation(jax.random.fold_in(stream_key, 2), number_of)[grade].astype(jnp.int32)


def normal_values(stream_key, extent, scale, bound, cuts=(), held_as=jnp.bfloat16):
    drawn = jax.random.normal(stream_key, extent, jnp.float32) * scale
    if len(cuts) > 0:
        drawn = block_levels(stream_key, extent, cuts, -0.22, 0.18) * drawn
    return jnp.clip(drawn, min=-bound, max=bound).astype(held_as)


def setup_inputs(seed: int = 0) -> dict:
    splits = jax.random.split(jax.random.key(seed), 14)
    return {
        "tokens": normal_values(splits[0], (TOKENS, MODEL_WIDTH), 1.0, 6.0, ((0, 16), (1, 16))),
        "cotangent": normal_values(splits[1], (TOKENS, MODEL_WIDTH), 0.04, 0.625, ((0, 16), (1, 16))),
        "gate_weight": normal_values(splits[2], (MODEL_WIDTH, FFW), MODEL_WIDTH ** -0.5, 0.0625, ((0, 16), (1, 16))),
        "up_weight": normal_values(splits[3], (MODEL_WIDTH, FFW), MODEL_WIDTH ** -0.5, 0.0625, ((0, 16), (1, 16))),
        "down_weight": normal_values(splits[4], (FFW, MODEL_WIDTH), FFW ** -0.5, 0.046875, ((0, 16), (1, 16))),
        "gate_in": normal_values(splits[5], (TENANTS, MODEL_WIDTH, R), MODEL_WIDTH ** -0.5, 0.0625, ((1, 16),)),
        "up_in": normal_values(splits[6], (TENANTS, MODEL_WIDTH, R), MODEL_WIDTH ** -0.5, 0.0625, ((1, 16),)),
        "down_out": normal_values(splits[7], (TENANTS, R, MODEL_WIDTH), R ** -0.5, 1.5, ((2, 16),)),
        "gate_out": normal_values(splits[8], (TENANTS, R, FFW), R ** -0.5, 1.5, ((2, 16),)),
        "up_out": normal_values(splits[9], (TENANTS, R, FFW), R ** -0.5, 1.5, ((2, 16),)),
        "down_in": normal_values(splits[10], (TENANTS, FFW, R), FFW ** -0.5, 0.046875, ((1, 16),)),
        "tenants": set_ends(ranked(splits[11], (NBLK,), TENANTS, 2), jax.random.fold_in(splits[11], 3), 0, TENANTS - 1).astype(jnp.int32),
        "owners": jax.random.permutation(splits[12], TENANTS).astype(jnp.int32),
    }


adapter_scale = 0.5


def split_product(left, right, pieces):
    width = left.shape[1] // pieces
    total = jnp.zeros((left.shape[0], right.shape[1]), jnp.float32)
    for piece in range(pieces):
        term = jnp.dot(left[:, piece * width:(piece + 1) * width], right[piece * width:(piece + 1) * width], preferred_element_type=jnp.float32)
        term = lax.optimization_barrier(term.astype(jnp.bfloat16))
        total = total + term.astype(jnp.float32)
    return total


def split_product_back(left, right, pieces):
    width = left.shape[1] // pieces
    total = jnp.zeros((left.shape[0], right.shape[0]), jnp.float32)
    for piece in range(pieces):
        term = lax.dot_general(left[:, piece * width:(piece + 1) * width], right[:, piece * width:(piece + 1) * width], (((1,), (1,)), ((), ())), preferred_element_type=jnp.float32)
        term = lax.optimization_barrier(term.astype(jnp.bfloat16))
        total = total + term.astype(jnp.float32)
    return total


def split_rank(left_blocks, chosen, pieces):
    width = left_blocks.shape[2] // pieces
    total = jnp.zeros((left_blocks.shape[0], left_blocks.shape[1], chosen.shape[2]), jnp.float32)
    for piece in range(pieces):
        term = jnp.einsum("btk,bkr->btr", left_blocks[:, :, piece * width:(piece + 1) * width].astype(jnp.float32), chosen[:, piece * width:(piece + 1) * width].astype(jnp.float32))
        term = lax.optimization_barrier(term.astype(jnp.bfloat16))
        total = total + term.astype(jnp.float32)
    return total


def reference(tokens, cotangent, gate_weight, up_weight, down_weight, gate_in, up_in, down_out, gate_out, up_out, down_in, tenants, owners):
    highest = lax.Precision.HIGHEST
    blocks_all = tenants.shape[0]
    every_token_row = tokens.shape[0]
    input_blocks = tokens.reshape(blocks_all, BLOCK, MODEL_WIDTH)
    gate_frozen_term = split_product(tokens, gate_weight, N_DP).reshape(blocks_all, BLOCK, FFW)
    up_frozen_term = split_product(tokens, up_weight, N_DP).reshape(blocks_all, BLOCK, FFW)
    gate_rank_second = split_rank(input_blocks, gate_in[tenants], N_DP).astype(jnp.bfloat16).astype(jnp.float32)
    up_rank_second = split_rank(input_blocks, up_in[tenants], N_DP).astype(jnp.bfloat16).astype(jnp.float32)
    gate_raise = gate_out[tenants].astype(jnp.float32)
    up_raise = up_out[tenants].astype(jnp.float32)
    gate_complete = gate_frozen_term + adapter_scale * jnp.einsum("uim,umn->uin", gate_rank_second, gate_raise)
    up_complete = up_frozen_term + adapter_scale * jnp.einsum("uim,umn->uin", up_rank_second, up_raise)
    hidden = (jax.nn.silu(gate_complete) * up_complete).astype(jnp.bfloat16)
    output_frozen_term = split_product(hidden.reshape(every_token_row, FFW), down_weight, N_TENSOR).reshape(blocks_all, BLOCK, MODEL_WIDTH)
    down_rank_second = split_rank(hidden, down_in[tenants], N_TENSOR).astype(jnp.bfloat16).astype(jnp.float32)
    down_raise = down_out[tenants].astype(jnp.float32)
    mixed = (output_frozen_term + adapter_scale * jnp.einsum("vmn,vnx->vmx", down_rank_second, down_raise)).astype(jnp.bfloat16).reshape(every_token_row, MODEL_WIDTH)

    cotangent_block_list = cotangent.reshape(blocks_all, BLOCK, MODEL_WIDTH).astype(jnp.float32)
    down_backward = (adapter_scale * jnp.einsum("env,ejv->enj", cotangent_block_list, down_raise)).astype(jnp.bfloat16).astype(jnp.float32)
    tenant_ids = jnp.arange(TENANTS, dtype=jnp.int32)
    tenant_onehot = (tenant_ids[:, None] == tenants[None, :]).astype(jnp.float32)
    slot_onehot = (tenant_ids[:, None] == owners[tenants][None, :]).astype(jnp.float32)
    raise_block_list = adapter_scale * jnp.einsum("jpy,jpz->jyz", down_rank_second, cotangent_block_list)
    grad_down_out = jnp.einsum("eb,brd->erd", tenant_onehot, raise_block_list, precision=highest)
    hidden_grad = split_product_back(cotangent, down_weight, N_DP).reshape(blocks_all, BLOCK, FFW)
    hidden_grad = hidden_grad + jnp.einsum("btr,bfr->btf", down_backward, down_in[tenants].astype(jnp.float32))
    sig = jax.nn.sigmoid(gate_complete)
    up_gradient = (hidden_grad * gate_complete * sig).astype(jnp.bfloat16).astype(jnp.float32)
    gate_gradient = (hidden_grad * up_complete * sig * (1.0 + gate_complete * (1.0 - sig))).astype(jnp.bfloat16).astype(jnp.float32)
    gate_backward = (adapter_scale * jnp.einsum("yae,yve->yav", gate_gradient, gate_raise)).astype(jnp.bfloat16).astype(jnp.float32)
    up_backward = (adapter_scale * jnp.einsum("yae,yve->yav", up_gradient, up_raise)).astype(jnp.bfloat16).astype(jnp.float32)
    input_float = input_blocks.astype(jnp.float32)
    grad_gate_in = jnp.einsum("eb,bdr->edr", tenant_onehot, jnp.einsum("btd,btr->bdr", input_float, gate_backward), precision=highest)
    grad_up_in = jnp.einsum("eb,bdr->edr", tenant_onehot, jnp.einsum("btd,btr->bdr", input_float, up_backward), precision=highest)
    gate_raise_block_list = adapter_scale * jnp.einsum("yap,yau->ypu", gate_rank_second, gate_gradient)
    up_raise_block_list = adapter_scale * jnp.einsum("yap,yau->ypu", up_rank_second, up_gradient)
    grad_gate_out = jnp.einsum("sb,brf->srf", slot_onehot, gate_raise_block_list, precision=highest)
    grad_up_out = jnp.einsum("sb,brf->srf", slot_onehot, up_raise_block_list, precision=highest)
    drop_blocks = jnp.einsum("btf,btr->bfr", hidden.astype(jnp.float32), down_backward)
    grad_down_in = jnp.einsum("sb,bfr->sfr", slot_onehot, drop_blocks, precision=highest)
    return (mixed, grad_gate_in, grad_up_in, grad_down_out, grad_gate_out, grad_up_out, grad_down_in)
```

```python
import jax
import jax.numpy as jnp
from jax import lax
from jax.sharding import PartitionSpec as P

BLOCK = 64


adapter_scale = 0.5


def scatter_sum(x, axis):
    count = lax.axis_size(axis)
    pieces = x.astype(jnp.bfloat16).reshape((count, x.shape[0] // count) + x.shape[1:])
    got = lax.all_to_all(pieces, axis, 0, 0, tiled=False)
    return got.astype(jnp.float32).sum(0)


def gather_rows(x, axis):
    count = lax.axis_size(axis)
    got = lax.all_to_all(jnp.broadcast_to(x[None], (count,) + x.shape), axis, 0, 0, tiled=False)
    return got.reshape((count * x.shape[0],) + x.shape[1:])


def shards(
    tokens,
    cotangent,
    gate_weight,
    up_weight,
    down_weight,
    gate_in,
    up_in,
    down_out,
    gate_out,
    up_out,
    down_in,
    tenants,
    owners,
):
    highest = lax.Precision.HIGHEST
    dp_count = lax.axis_size("dp")
    tensor_count = lax.axis_size("tensor")
    dp_index = lax.axis_index("dp")
    tensor_index = lax.axis_index("tensor")
    rows_in = tokens.shape[0]
    feat_here = tokens.shape[1]
    width_here = gate_weight.shape[1]
    rank_width = gate_in.shape[2]
    every_token_row = rows_in * tensor_count
    group_rows = every_token_row // dp_count
    blocks_all = tenants.shape[0]
    blocks_group = group_rows // BLOCK
    blocks_in = rows_in // BLOCK
    tenant_count = owners.shape[0]
    slots_here = tenant_count // dp_count
    tenants_here = tenant_count // tensor_count
    group_tenants = lax.dynamic_slice_in_dim(tenants, dp_index * blocks_group, blocks_group)
    input_tenants = lax.dynamic_slice_in_dim(tenants, tensor_index * blocks_in, blocks_in)
    contract_rows = (((0,), (0,)), ((), ()))
    token_tenants = jnp.broadcast_to(tenants[:, None], (blocks_all, BLOCK)).reshape(every_token_row)
    held_tenants = tensor_index * tenants_here + jnp.arange(tenants_here, dtype=jnp.int32)
    token_onehot = (token_tenants[:, None] == held_tenants[None, :]).astype(jnp.bfloat16)
    all_inputs = lax.all_gather(tokens, "tensor", axis=0, tiled=True)
    all_cot = lax.all_gather(cotangent, "tensor", axis=0, tiled=True)

    gate_part = jnp.dot(all_inputs, gate_weight, preferred_element_type=jnp.float32)
    up_part = jnp.dot(all_inputs, up_weight, preferred_element_type=jnp.float32)
    input_blocks = all_inputs.reshape(blocks_all, BLOCK, feat_here)
    gate_rank_part = jnp.einsum(
        "btk,bkr->btr", input_blocks, gate_in[tenants], preferred_element_type=jnp.float32
    ).reshape(every_token_row, rank_width)
    up_rank_part = jnp.einsum(
        "btk,bkr->btr", input_blocks, up_in[tenants], preferred_element_type=jnp.float32
    ).reshape(every_token_row, rank_width)
    forward_sums = scatter_sum(
        jnp.concatenate(
            [
                gate_part.astype(jnp.bfloat16),
                up_part.astype(jnp.bfloat16),
                gate_rank_part.astype(jnp.bfloat16),
                up_rank_part.astype(jnp.bfloat16),
            ],
            axis=1,
        ),
        "dp",
    )
    gate_total_sum = forward_sums[:, :width_here]
    up_total_sum = forward_sums[:, width_here : 2 * width_here]
    gate_rank = forward_sums[:, 2 * width_here : 2 * width_here + rank_width]
    up_rank = forward_sums[:, 2 * width_here + rank_width :]
    gate_rank_second = gate_rank.astype(jnp.bfloat16).reshape(blocks_group, BLOCK, rank_width)
    up_rank_second = up_rank.astype(jnp.bfloat16).reshape(blocks_group, BLOCK, rank_width)
    gate_raise = gate_out[group_tenants]
    up_raise = up_out[group_tenants]
    gate_complete = gate_total_sum + adapter_scale * jnp.einsum(
        "uim,umn->uin", gate_rank_second, gate_raise, preferred_element_type=jnp.float32
    ).reshape(group_rows, width_here)
    up_complete = up_total_sum + adapter_scale * jnp.einsum(
        "uim,umn->uin", up_rank_second, up_raise, preferred_element_type=jnp.float32
    ).reshape(group_rows, width_here)
    hidden = (jax.nn.silu(gate_complete) * up_complete).astype(jnp.bfloat16)
    all_hidden = gather_rows(hidden, "dp")

    out_part = jnp.dot(all_hidden, down_weight, preferred_element_type=jnp.float32)
    down_rank_part = jnp.einsum(
        "btf,bfr->btr",
        all_hidden.reshape(blocks_all, BLOCK, width_here),
        down_in[tenants],
        preferred_element_type=jnp.float32,
    ).reshape(every_token_row, rank_width)
    down_sums = scatter_sum(
        jnp.concatenate(
            [out_part.astype(jnp.bfloat16), down_rank_part.astype(jnp.bfloat16)], axis=1
        ),
        "tensor",
    )
    out_sum = down_sums[:, :feat_here]
    down_rank_flat = down_sums[:, feat_here:].astype(jnp.bfloat16)
    down_rank_second = down_rank_flat.reshape(blocks_in, BLOCK, rank_width)
    down_raise = down_out[input_tenants]
    mixed = (
        out_sum
        + adapter_scale
        * jnp.einsum(
            "vmn,vnx->vmx", down_rank_second, down_raise, preferred_element_type=jnp.float32
        ).reshape(rows_in, feat_here)
    ).astype(jnp.bfloat16)

    all_down_rank = lax.all_gather(down_rank_flat, "tensor", axis=0, tiled=True)
    rank_weighted = (token_onehot[:, :, None] * all_down_rank[:, None, :]).reshape(
        every_token_row, tenants_here * rank_width
    )
    grad_down_out = adapter_scale * (
        lax.dot_general(rank_weighted, all_cot, contract_rows, preferred_element_type=jnp.float32)
        .reshape(tenants_here, rank_width, feat_here)
    )

    hidden_grad_part = lax.dot_general(
        all_cot, down_weight, (((1,), (1,)), ((), ())), preferred_element_type=jnp.float32
    )
    down_back_part = adapter_scale * jnp.einsum(
        "env,ejv->enj",
        all_cot.reshape(blocks_all, BLOCK, feat_here),
        down_out[tenants],
        preferred_element_type=jnp.float32,
    ).reshape(every_token_row, rank_width)
    back_sums = scatter_sum(
        jnp.concatenate(
            [hidden_grad_part.astype(jnp.bfloat16), down_back_part.astype(jnp.bfloat16)], axis=1
        ),
        "dp",
    )
    hidden_grad_sum = back_sums[:, :width_here]
    group_down_back = back_sums[:, width_here:].astype(jnp.bfloat16)
    down_drop = down_in[group_tenants]
    hidden_grad = hidden_grad_sum + jnp.einsum(
        "btr,bfr->btf",
        group_down_back.reshape(blocks_group, BLOCK, rank_width),
        down_drop,
        preferred_element_type=jnp.float32,
    ).reshape(group_rows, width_here)
    sig = jax.nn.sigmoid(gate_complete)
    up_gradient = (
        (hidden_grad * gate_complete * sig)
        .astype(jnp.bfloat16)
        .reshape(blocks_group, BLOCK, width_here)
    )
    gate_gradient = (
        (hidden_grad * up_complete * sig * (1.0 + gate_complete * (1.0 - sig)))
        .astype(jnp.bfloat16)
        .reshape(blocks_group, BLOCK, width_here)
    )
    gate_backward_piece = adapter_scale * jnp.einsum(
        "yae,yve->yav", gate_gradient, gate_raise, preferred_element_type=jnp.float32
    )
    up_backward_piece = adapter_scale * jnp.einsum(
        "yae,yve->yav", up_gradient, up_raise, preferred_element_type=jnp.float32
    )
    gate_backward, up_backward = lax.psum((gate_backward_piece, up_backward_piece), "tensor")

    gate_raise_block_list = adapter_scale * jnp.einsum(
        "yap,yau->ypu", gate_rank_second, gate_gradient, preferred_element_type=jnp.float32
    )
    up_raise_block_list = adapter_scale * jnp.einsum(
        "yap,yau->ypu", up_rank_second, up_gradient, preferred_element_type=jnp.float32
    )
    all_raise_blocks = gather_rows(
        jnp.stack([gate_raise_block_list, up_raise_block_list], axis=1).astype(jnp.bfloat16),
        "dp",
    ).astype(jnp.float32)
    own_slots = dp_index * slots_here + jnp.arange(slots_here, dtype=jnp.int32)
    block_onehot = (own_slots[:, None] == owners[tenants][None, :]).astype(jnp.float32)
    grad_gate_out = jnp.einsum(
        "sb,brf->srf", block_onehot, all_raise_blocks[:, 0], precision=highest
    )
    grad_up_out = jnp.einsum("sb,brf->srf", block_onehot, all_raise_blocks[:, 1], precision=highest)

    all_backs = lax.all_gather(
        jnp.concatenate(
            [
                gate_backward.astype(jnp.bfloat16).reshape(group_rows, rank_width),
                up_backward.astype(jnp.bfloat16).reshape(group_rows, rank_width),
                group_down_back,
            ],
            axis=1,
        ),
        "dp",
        axis=0,
        tiled=True,
    )
    all_gate_back = all_backs[:, :rank_width]
    all_up_back = all_backs[:, rank_width : 2 * rank_width]
    all_down_back = all_backs[:, 2 * rank_width :]
    gate_weighted = (token_onehot[:, :, None] * all_gate_back[:, None, :]).reshape(
        every_token_row, tenants_here * rank_width
    )
    up_weighted = (token_onehot[:, :, None] * all_up_back[:, None, :]).reshape(
        every_token_row, tenants_here * rank_width
    )
    grad_gate_in = (
        lax.dot_general(
            all_inputs, gate_weighted, contract_rows, preferred_element_type=jnp.float32
        )
        .reshape(feat_here, tenants_here, rank_width)
        .transpose(1, 0, 2)
    )
    grad_up_in = (
        lax.dot_general(all_inputs, up_weighted, contract_rows, preferred_element_type=jnp.float32)
        .reshape(feat_here, tenants_here, rank_width)
        .transpose(1, 0, 2)
    )
    token_slots = owners[token_tenants]
    slot_onehot = (token_slots[:, None] == own_slots[None, :]).astype(jnp.bfloat16)
    drop_weighted = (slot_onehot[:, :, None] * all_down_back[:, None, :]).reshape(
        every_token_row, slots_here * rank_width
    )
    grad_down_in = (
        lax.dot_general(
            all_hidden, drop_weighted, contract_rows, preferred_element_type=jnp.float32
        )
        .reshape(width_here, slots_here, rank_width)
        .transpose(1, 0, 2)
    )
    return (
        mixed,
        grad_gate_in,
        grad_up_in,
        grad_down_out,
        grad_gate_out,
        grad_up_out,
        grad_down_in,
    )


def solution(mesh):
    in_specs = (
        P("tensor", "dp"),
        P("tensor", "dp"),
        P("dp", "tensor"),
        P("dp", "tensor"),
        P("tensor", "dp"),
        P(None, "dp", None),
        P(None, "dp", None),
        P(None, None, "dp"),
        P(None, None, "tensor"),
        P(None, None, "tensor"),
        P(None, "tensor", None),
        P(),
        P(),
    )
    out_specs = (
        P("tensor", "dp"),
        P("tensor", "dp", None),
        P("tensor", "dp", None),
        P("tensor", None, "dp"),
        P("dp", None, "tensor"),
        P("dp", None, "tensor"),
        P("dp", "tensor", None),
    )
    return jax.shard_map(shards, mesh=mesh, in_specs=in_specs, out_specs=out_specs, check_vma=False)
```

```python
import jax
import jax.numpy as jnp
from jax import lax
from jax.sharding import PartitionSpec as P

BLOCK = 64


adapter_scale = 0.5


def scatter_sum(x, axis):
    count = lax.axis_size(axis)
    pieces = x.astype(jnp.bfloat16).reshape((count, x.shape[0] // count) + x.shape[1:])
    got = lax.all_to_all(pieces, axis, 0, 0, tiled=False)
    return got.astype(jnp.float32).sum(0)


def gather_rows(x, axis):
    count = lax.axis_size(axis)
    got = lax.all_to_all(jnp.broadcast_to(x[None], (count,) + x.shape), axis, 0, 0, tiled=False)
    return got.reshape((count * x.shape[0],) + x.shape[1:])


def shards(
    tokens,
    cotangent,
    gate_weight,
    up_weight,
    down_weight,
    gate_in,
    up_in,
    down_out,
    gate_out,
    up_out,
    down_in,
    tenants,
    owners,
):
    highest = lax.Precision.HIGHEST
    dp_count = lax.axis_size("dp")
    tensor_count = lax.axis_size("tensor")
    dp_index = lax.axis_index("dp")
    tensor_index = lax.axis_index("tensor")
    rows_in = tokens.shape[0]
    feat_here = tokens.shape[1]
    width_here = gate_weight.shape[1]
    rank_width = gate_in.shape[2]
    every_token_row = rows_in * tensor_count
    group_rows = every_token_row // dp_count
    blocks_all = tenants.shape[0]
    blocks_group = group_rows // BLOCK
    blocks_in = rows_in // BLOCK
    tenant_count = owners.shape[0]
    slots_here = tenant_count // dp_count
    tenants_here = tenant_count // tensor_count
    group_tenants = lax.dynamic_slice_in_dim(tenants, dp_index * blocks_group, blocks_group)
    input_tenants = lax.dynamic_slice_in_dim(tenants, tensor_index * blocks_in, blocks_in)
    contract_rows = (((0,), (0,)), ((), ()))
    token_tenants = jnp.broadcast_to(tenants[:, None], (blocks_all, BLOCK)).reshape(every_token_row)
    held_tenants = tensor_index * tenants_here + jnp.arange(tenants_here, dtype=jnp.int32)
    token_onehot = (token_tenants[:, None] == held_tenants[None, :]).astype(jnp.bfloat16)
    all_inputs = lax.all_gather(tokens, "tensor", axis=0, tiled=True)
    cotangent = lax.optimization_barrier((all_inputs, cotangent))[1]
    all_cot = lax.all_gather(cotangent, "tensor", axis=0, tiled=True)

    gate_part = jnp.dot(all_inputs, gate_weight, preferred_element_type=jnp.float32)
    up_part = jnp.dot(all_inputs, up_weight, preferred_element_type=jnp.float32)
    input_blocks = all_inputs.reshape(blocks_all, BLOCK, feat_here)
    gate_rank_part = jnp.einsum(
        "btk,bkr->btr", input_blocks, gate_in[tenants], preferred_element_type=jnp.float32
    ).reshape(every_token_row, rank_width)
    up_rank_part = jnp.einsum(
        "btk,bkr->btr", input_blocks, up_in[tenants], preferred_element_type=jnp.float32
    ).reshape(every_token_row, rank_width)
    forward_sums = scatter_sum(
        jnp.concatenate(
            [
                gate_part.astype(jnp.bfloat16),
                up_part.astype(jnp.bfloat16),
                gate_rank_part.astype(jnp.bfloat16),
                up_rank_part.astype(jnp.bfloat16),
            ],
            axis=1,
        ),
        "dp",
    )
    gate_total_sum = forward_sums[:, :width_here]
    up_total_sum = forward_sums[:, width_here : 2 * width_here]
    gate_rank = forward_sums[:, 2 * width_here : 2 * width_here + rank_width]
    up_rank = forward_sums[:, 2 * width_here + rank_width :]
    gate_rank_second = gate_rank.astype(jnp.bfloat16).reshape(blocks_group, BLOCK, rank_width)
    up_rank_second = up_rank.astype(jnp.bfloat16).reshape(blocks_group, BLOCK, rank_width)
    gate_raise = gate_out[group_tenants]
    up_raise = up_out[group_tenants]
    gate_complete = gate_total_sum + adapter_scale * jnp.einsum(
        "uim,umn->uin", gate_rank_second, gate_raise, preferred_element_type=jnp.float32
    ).reshape(group_rows, width_here)
    up_complete = up_total_sum + adapter_scale * jnp.einsum(
        "uim,umn->uin", up_rank_second, up_raise, preferred_element_type=jnp.float32
    ).reshape(group_rows, width_here)
    hidden = (jax.nn.silu(gate_complete) * up_complete).astype(jnp.bfloat16)
    all_hidden = gather_rows(hidden, "dp")

    out_part = jnp.dot(all_hidden, down_weight, preferred_element_type=jnp.float32)
    down_rank_part = jnp.einsum(
        "btf,bfr->btr",
        all_hidden.reshape(blocks_all, BLOCK, width_here),
        down_in[tenants],
        preferred_element_type=jnp.float32,
    ).reshape(every_token_row, rank_width)
    down_sums = scatter_sum(
        jnp.concatenate(
            [out_part.astype(jnp.bfloat16), down_rank_part.astype(jnp.bfloat16)], axis=1
        ),
        "tensor",
    )
    out_sum = down_sums[:, :feat_here]
    down_rank_flat = down_sums[:, feat_here:].astype(jnp.bfloat16)
    down_rank_second = down_rank_flat.reshape(blocks_in, BLOCK, rank_width)
    down_raise = down_out[input_tenants]
    mixed = (
        out_sum
        + adapter_scale
        * jnp.einsum(
            "vmn,vnx->vmx", down_rank_second, down_raise, preferred_element_type=jnp.float32
        ).reshape(rows_in, feat_here)
    ).astype(jnp.bfloat16)

    hidden_grad_part = lax.dot_general(
        all_cot, down_weight, (((1,), (1,)), ((), ())), preferred_element_type=jnp.float32
    )
    down_back_part = adapter_scale * jnp.einsum(
        "env,ejv->enj",
        all_cot.reshape(blocks_all, BLOCK, feat_here),
        down_out[tenants],
        preferred_element_type=jnp.float32,
    ).reshape(every_token_row, rank_width)
    back_pieces = jnp.concatenate(
        [hidden_grad_part.astype(jnp.bfloat16), down_back_part.astype(jnp.bfloat16)], axis=1
    )
    forward_sums, back_pieces = lax.optimization_barrier((forward_sums, back_pieces))
    back_sums = scatter_sum(back_pieces, "dp")
    hidden_grad_sum = back_sums[:, :width_here]
    group_down_back = back_sums[:, width_here:].astype(jnp.bfloat16)
    down_drop = down_in[group_tenants]
    hidden_grad = hidden_grad_sum + jnp.einsum(
        "btr,bfr->btf",
        group_down_back.reshape(blocks_group, BLOCK, rank_width),
        down_drop,
        preferred_element_type=jnp.float32,
    ).reshape(group_rows, width_here)
    sig = jax.nn.sigmoid(gate_complete)
    up_gradient = (
        (hidden_grad * gate_complete * sig)
        .astype(jnp.bfloat16)
        .reshape(blocks_group, BLOCK, width_here)
    )
    gate_gradient = (
        (hidden_grad * up_complete * sig * (1.0 + gate_complete * (1.0 - sig)))
        .astype(jnp.bfloat16)
        .reshape(blocks_group, BLOCK, width_here)
    )
    gate_backward_piece = adapter_scale * jnp.einsum(
        "yae,yve->yav", gate_gradient, gate_raise, preferred_element_type=jnp.float32
    )
    up_backward_piece = adapter_scale * jnp.einsum(
        "yae,yve->yav", up_gradient, up_raise, preferred_element_type=jnp.float32
    )
    rank_partials = lax.all_gather(
        jnp.concatenate(
            [
                gate_backward_piece.reshape(group_rows, rank_width),
                up_backward_piece.reshape(group_rows, rank_width),
                down_rank_flat.astype(jnp.float32),
            ],
            axis=1,
        ),
        "tensor",
        axis=0,
        tiled=False,
    )
    back_rank_sums = rank_partials[:, :, : 2 * rank_width].sum(0)
    gate_backward = back_rank_sums[:, :rank_width]
    up_backward = back_rank_sums[:, rank_width:]
    all_down_rank = rank_partials[:, :, 2 * rank_width :].reshape(every_token_row, rank_width)
    rank_weighted = (token_onehot[:, :, None] * all_down_rank[:, None, :]).reshape(
        every_token_row, tenants_here * rank_width
    )
    grad_down_out = adapter_scale * (
        lax.dot_general(rank_weighted, all_cot, contract_rows, preferred_element_type=jnp.float32)
        .reshape(tenants_here, rank_width, feat_here)
    )

    gate_raise_block_list = adapter_scale * jnp.einsum(
        "yap,yau->ypu", gate_rank_second, gate_gradient, preferred_element_type=jnp.float32
    )
    up_raise_block_list = adapter_scale * jnp.einsum(
        "yap,yau->ypu", up_rank_second, up_gradient, preferred_element_type=jnp.float32
    )
    all_raise_blocks = gather_rows(
        jnp.stack([gate_raise_block_list, up_raise_block_list], axis=1).astype(jnp.bfloat16),
        "dp",
    ).astype(jnp.float32)
    own_slots = dp_index * slots_here + jnp.arange(slots_here, dtype=jnp.int32)
    block_onehot = (own_slots[:, None] == owners[tenants][None, :]).astype(jnp.float32)
    grad_gate_out = jnp.einsum(
        "sb,brf->srf", block_onehot, all_raise_blocks[:, 0], precision=highest
    )
    grad_up_out = jnp.einsum("sb,brf->srf", block_onehot, all_raise_blocks[:, 1], precision=highest)

    all_backs = lax.all_gather(
        jnp.concatenate(
            [
                gate_backward.astype(jnp.bfloat16),
                up_backward.astype(jnp.bfloat16),
                group_down_back,
            ],
            axis=1,
        ),
        "dp",
        axis=0,
        tiled=True,
    )
    all_gate_back = all_backs[:, :rank_width]
    all_up_back = all_backs[:, rank_width : 2 * rank_width]
    all_down_back = all_backs[:, 2 * rank_width :]
    gate_weighted = (token_onehot[:, :, None] * all_gate_back[:, None, :]).reshape(
        every_token_row, tenants_here * rank_width
    )
    up_weighted = (token_onehot[:, :, None] * all_up_back[:, None, :]).reshape(
        every_token_row, tenants_here * rank_width
    )
    grad_gate_in = (
        lax.dot_general(
            all_inputs, gate_weighted, contract_rows, preferred_element_type=jnp.float32
        )
        .reshape(feat_here, tenants_here, rank_width)
        .transpose(1, 0, 2)
    )
    grad_up_in = (
        lax.dot_general(all_inputs, up_weighted, contract_rows, preferred_element_type=jnp.float32)
        .reshape(feat_here, tenants_here, rank_width)
        .transpose(1, 0, 2)
    )
    block_slot_onehot = (owners[tenants][:, None] == own_slots[None, :]).astype(jnp.bfloat16)
    slot_onehot = jnp.broadcast_to(
        block_slot_onehot[:, None, :], (blocks_all, BLOCK, slots_here)
    ).reshape(every_token_row, slots_here)
    drop_weighted = (slot_onehot[:, :, None] * all_down_back[:, None, :]).reshape(
        every_token_row, slots_here * rank_width
    )
    grad_down_in = (
        lax.dot_general(
            all_hidden, drop_weighted, contract_rows, preferred_element_type=jnp.float32
        )
        .reshape(width_here, slots_here, rank_width)
        .transpose(1, 0, 2)
    )
    return (
        mixed,
        grad_gate_in,
        grad_up_in,
        grad_down_out,
        grad_gate_out,
        grad_up_out,
        grad_down_in,
    )


def solution(mesh):
    in_specs = (
        P("tensor", "dp"),
        P("tensor", "dp"),
        P("dp", "tensor"),
        P("dp", "tensor"),
        P("tensor", "dp"),
        P(None, "dp", None),
        P(None, "dp", None),
        P(None, None, "dp"),
        P(None, None, "tensor"),
        P(None, None, "tensor"),
        P(None, "tensor", None),
        P(),
        P(),
    )
    out_specs = (
        P("tensor", "dp"),
        P("tensor", "dp", None),
        P("tensor", "dp", None),
        P("tensor", None, "dp"),
        P("dp", None, "tensor"),
        P("dp", None, "tensor"),
        P("dp", "tensor", None),
    )
    return jax.shard_map(shards, mesh=mesh, in_specs=in_specs, out_specs=out_specs, check_vma=False)
```

```python
import jax
import jax.numpy as jnp
from jax import lax
from jax.sharding import PartitionSpec as P

BLOCK = 64


adapter_scale = 0.5


def scatter_sum(x, axis):
    count = lax.axis_size(axis)
    pieces = x.astype(jnp.bfloat16).reshape((count, x.shape[0] // count) + x.shape[1:])
    got = lax.all_to_all(pieces, axis, 0, 0, tiled=False)
    return got.astype(jnp.float32).sum(0)


def gather_rows(x, axis):
    count = lax.axis_size(axis)
    got = lax.all_to_all(jnp.broadcast_to(x[None], (count,) + x.shape), axis, 0, 0, tiled=False)
    return got.reshape((count * x.shape[0],) + x.shape[1:])


TENSOR = ("tz", "tc")


def gather_tensor(x):
    along_z = lax.all_gather(x, "tz", axis=0, tiled=False)
    both = lax.all_gather(along_z, "tc", axis=1, tiled=False)
    return both.reshape((-1,) + x.shape[1:])


def scatter_sum_tensor(x):
    count_z = lax.axis_size("tz")
    count_c = lax.axis_size("tc")
    pieces = x.astype(jnp.bfloat16).reshape(
        (count_z, count_c, x.shape[0] // (count_z * count_c)) + x.shape[1:]
    )
    pair = lax.all_to_all(pieces, "tc", 1, 1, tiled=False).astype(jnp.float32).sum(1)
    got = lax.all_to_all(pair.astype(jnp.bfloat16), "tz", 0, 0, tiled=False)
    return got.astype(jnp.float32).sum(0)


def shards(
    tokens,
    cotangent,
    gate_weight,
    up_weight,
    down_weight,
    gate_in,
    up_in,
    down_out,
    gate_out,
    up_out,
    down_in,
    tenants,
    owners,
):
    highest = lax.Precision.HIGHEST
    dp_count = lax.axis_size("dp")
    tensor_count = lax.axis_size("tz") * lax.axis_size("tc")
    dp_index = lax.axis_index("dp")
    tensor_index = lax.axis_index("tz") * lax.axis_size("tc") + lax.axis_index("tc")
    rows_in = tokens.shape[0]
    feat_here = tokens.shape[1]
    width_here = gate_weight.shape[1]
    rank_width = gate_in.shape[2]
    every_token_row = rows_in * tensor_count
    group_rows = every_token_row // dp_count
    blocks_all = tenants.shape[0]
    blocks_group = group_rows // BLOCK
    blocks_in = rows_in // BLOCK
    tenant_count = owners.shape[0]
    slots_here = tenant_count // dp_count
    tenants_here = tenant_count // tensor_count
    group_tenants = lax.dynamic_slice_in_dim(tenants, dp_index * blocks_group, blocks_group)
    input_tenants = lax.dynamic_slice_in_dim(tenants, tensor_index * blocks_in, blocks_in)
    contract_rows = (((0,), (0,)), ((), ()))
    token_tenants = jnp.broadcast_to(tenants[:, None], (blocks_all, BLOCK)).reshape(every_token_row)
    held_tenants = tensor_index * tenants_here + jnp.arange(tenants_here, dtype=jnp.int32)
    token_onehot = (token_tenants[:, None] == held_tenants[None, :]).astype(jnp.bfloat16)
    all_inputs = gather_tensor(tokens)
    cotangent = lax.optimization_barrier((all_inputs, cotangent))[1]
    all_cot = gather_tensor(cotangent)

    gate_part = jnp.dot(all_inputs, gate_weight, preferred_element_type=jnp.float32)
    up_part = jnp.dot(all_inputs, up_weight, preferred_element_type=jnp.float32)
    input_blocks = all_inputs.reshape(blocks_all, BLOCK, feat_here)
    gate_rank_part = jnp.einsum(
        "btk,bkr->btr", input_blocks, gate_in[tenants], preferred_element_type=jnp.float32
    ).reshape(every_token_row, rank_width)
    up_rank_part = jnp.einsum(
        "btk,bkr->btr", input_blocks, up_in[tenants], preferred_element_type=jnp.float32
    ).reshape(every_token_row, rank_width)
    forward_sums = scatter_sum(
        jnp.concatenate(
            [
                gate_part.astype(jnp.bfloat16),
                up_part.astype(jnp.bfloat16),
                gate_rank_part.astype(jnp.bfloat16),
                up_rank_part.astype(jnp.bfloat16),
            ],
            axis=1,
        ),
        "dp",
    )
    gate_total_sum = forward_sums[:, :width_here]
    up_total_sum = forward_sums[:, width_here : 2 * width_here]
    gate_rank = forward_sums[:, 2 * width_here : 2 * width_here + rank_width]
    up_rank = forward_sums[:, 2 * width_here + rank_width :]
    gate_rank_second = gate_rank.astype(jnp.bfloat16).reshape(blocks_group, BLOCK, rank_width)
    up_rank_second = up_rank.astype(jnp.bfloat16).reshape(blocks_group, BLOCK, rank_width)
    gate_raise = gate_out[group_tenants]
    up_raise = up_out[group_tenants]
    gate_complete = gate_total_sum + adapter_scale * jnp.einsum(
        "uim,umn->uin", gate_rank_second, gate_raise, preferred_element_type=jnp.float32
    ).reshape(group_rows, width_here)
    up_complete = up_total_sum + adapter_scale * jnp.einsum(
        "uim,umn->uin", up_rank_second, up_raise, preferred_element_type=jnp.float32
    ).reshape(group_rows, width_here)
    hidden = (jax.nn.silu(gate_complete) * up_complete).astype(jnp.bfloat16)
    all_hidden = gather_rows(hidden, "dp")

    out_part = jnp.dot(all_hidden, down_weight, preferred_element_type=jnp.float32)
    down_rank_part = jnp.einsum(
        "btf,bfr->btr",
        all_hidden.reshape(blocks_all, BLOCK, width_here),
        down_in[tenants],
        preferred_element_type=jnp.float32,
    ).reshape(every_token_row, rank_width)
    down_sums = scatter_sum_tensor(
        jnp.concatenate(
            [out_part.astype(jnp.bfloat16), down_rank_part.astype(jnp.bfloat16)], axis=1
        )
    )
    out_sum = down_sums[:, :feat_here]
    down_rank_flat = down_sums[:, feat_here:].astype(jnp.bfloat16)
    down_rank_second = down_rank_flat.reshape(blocks_in, BLOCK, rank_width)
    down_raise = down_out[input_tenants]
    mixed = (
        out_sum
        + adapter_scale
        * jnp.einsum(
            "vmn,vnx->vmx", down_rank_second, down_raise, preferred_element_type=jnp.float32
        ).reshape(rows_in, feat_here)
    ).astype(jnp.bfloat16)

    hidden_grad_part = lax.dot_general(
        all_cot, down_weight, (((1,), (1,)), ((), ())), preferred_element_type=jnp.float32
    )
    down_back_part = adapter_scale * jnp.einsum(
        "env,ejv->enj",
        all_cot.reshape(blocks_all, BLOCK, feat_here),
        down_out[tenants],
        preferred_element_type=jnp.float32,
    ).reshape(every_token_row, rank_width)
    back_pieces = jnp.concatenate(
        [hidden_grad_part.astype(jnp.bfloat16), down_back_part.astype(jnp.bfloat16)], axis=1
    )
    forward_sums, back_pieces = lax.optimization_barrier((forward_sums, back_pieces))
    back_sums = scatter_sum(back_pieces, "dp")
    hidden_grad_sum = back_sums[:, :width_here]
    group_down_back = back_sums[:, width_here:].astype(jnp.bfloat16)
    down_drop = down_in[group_tenants]
    hidden_grad = hidden_grad_sum + jnp.einsum(
        "btr,bfr->btf",
        group_down_back.reshape(blocks_group, BLOCK, rank_width),
        down_drop,
        preferred_element_type=jnp.float32,
    ).reshape(group_rows, width_here)
    sig = jax.nn.sigmoid(gate_complete)
    up_gradient = (
        (hidden_grad * gate_complete * sig)
        .astype(jnp.bfloat16)
        .reshape(blocks_group, BLOCK, width_here)
    )
    gate_gradient = (
        (hidden_grad * up_complete * sig * (1.0 + gate_complete * (1.0 - sig)))
        .astype(jnp.bfloat16)
        .reshape(blocks_group, BLOCK, width_here)
    )
    gate_backward_piece = adapter_scale * jnp.einsum(
        "yae,yve->yav", gate_gradient, gate_raise, preferred_element_type=jnp.float32
    )
    up_backward_piece = adapter_scale * jnp.einsum(
        "yae,yve->yav", up_gradient, up_raise, preferred_element_type=jnp.float32
    )
    rank_partials = lax.all_gather(
        jnp.concatenate(
            [
                gate_backward_piece.reshape(group_rows, rank_width),
                up_backward_piece.reshape(group_rows, rank_width),
                down_rank_flat.astype(jnp.float32),
            ],
            axis=1,
        ),
        TENSOR,
        axis=0,
        tiled=False,
    )
    back_rank_sums = rank_partials[:, :, : 2 * rank_width].sum(0)
    gate_backward = back_rank_sums[:, :rank_width]
    up_backward = back_rank_sums[:, rank_width:]
    all_down_rank = rank_partials[:, :, 2 * rank_width :].reshape(every_token_row, rank_width)
    rank_weighted = (token_onehot[:, :, None] * all_down_rank[:, None, :]).reshape(
        every_token_row, tenants_here * rank_width
    )
    grad_down_out = adapter_scale * (
        lax.dot_general(rank_weighted, all_cot, contract_rows, preferred_element_type=jnp.float32)
        .reshape(tenants_here, rank_width, feat_here)
    )

    gate_raise_block_list = adapter_scale * jnp.einsum(
        "yap,yau->ypu", gate_rank_second, gate_gradient, preferred_element_type=jnp.float32
    )
    up_raise_block_list = adapter_scale * jnp.einsum(
        "yap,yau->ypu", up_rank_second, up_gradient, preferred_element_type=jnp.float32
    )
    all_raise_blocks = gather_rows(
        jnp.stack([gate_raise_block_list, up_raise_block_list], axis=1).astype(jnp.bfloat16),
        "dp",
    ).astype(jnp.float32)
    own_slots = dp_index * slots_here + jnp.arange(slots_here, dtype=jnp.int32)
    block_onehot = (own_slots[:, None] == owners[tenants][None, :]).astype(jnp.float32)
    grad_gate_out = jnp.einsum(
        "sb,brf->srf", block_onehot, all_raise_blocks[:, 0], precision=highest
    )
    grad_up_out = jnp.einsum("sb,brf->srf", block_onehot, all_raise_blocks[:, 1], precision=highest)

    all_backs = lax.all_gather(
        jnp.concatenate(
            [
                gate_backward.astype(jnp.bfloat16),
                up_backward.astype(jnp.bfloat16),
                group_down_back,
            ],
            axis=1,
        ),
        "dp",
        axis=0,
        tiled=True,
    )
    all_gate_back = all_backs[:, :rank_width]
    all_up_back = all_backs[:, rank_width : 2 * rank_width]
    all_down_back = all_backs[:, 2 * rank_width :]
    gate_weighted = (token_onehot[:, :, None] * all_gate_back[:, None, :]).reshape(
        every_token_row, tenants_here * rank_width
    )
    up_weighted = (token_onehot[:, :, None] * all_up_back[:, None, :]).reshape(
        every_token_row, tenants_here * rank_width
    )
    grad_gate_in = (
        lax.dot_general(
            all_inputs, gate_weighted, contract_rows, preferred_element_type=jnp.float32
        )
        .reshape(feat_here, tenants_here, rank_width)
        .transpose(1, 0, 2)
    )
    grad_up_in = (
        lax.dot_general(all_inputs, up_weighted, contract_rows, preferred_element_type=jnp.float32)
        .reshape(feat_here, tenants_here, rank_width)
        .transpose(1, 0, 2)
    )
    block_slot_onehot = (owners[tenants][:, None] == own_slots[None, :]).astype(jnp.bfloat16)
    slot_onehot = jnp.broadcast_to(
        block_slot_onehot[:, None, :], (blocks_all, BLOCK, slots_here)
    ).reshape(every_token_row, slots_here)
    drop_weighted = (slot_onehot[:, :, None] * all_down_back[:, None, :]).reshape(
        every_token_row, slots_here * rank_width
    )
    grad_down_in = (
        lax.dot_general(
            all_hidden, drop_weighted, contract_rows, preferred_element_type=jnp.float32
        )
        .reshape(width_here, slots_here, rank_width)
        .transpose(1, 0, 2)
    )
    return (
        mixed,
        grad_gate_in,
        grad_up_in,
        grad_down_out,
        grad_gate_out,
        grad_up_out,
        grad_down_in,
    )


def solution(mesh):
    devices = mesh.devices.reshape(mesh.shape["dp"], mesh.shape["tensor"] // 2, 2)
    split_mesh = jax.sharding.Mesh(devices, ("dp",) + TENSOR)
    in_specs = (
        P(TENSOR, "dp"),
        P(TENSOR, "dp"),
        P("dp", TENSOR),
        P("dp", TENSOR),
        P(TENSOR, "dp"),
        P(None, "dp", None),
        P(None, "dp", None),
        P(None, None, "dp"),
        P(None, None, TENSOR),
        P(None, None, TENSOR),
        P(None, TENSOR, None),
        P(),
        P(),
    )
    out_specs = (
        P(TENSOR, "dp"),
        P(TENSOR, "dp", None),
        P(TENSOR, "dp", None),
        P(TENSOR, None, "dp"),
        P("dp", None, TENSOR),
        P("dp", None, TENSOR),
        P("dp", TENSOR, None),
    )
    return jax.shard_map(shards, mesh=split_mesh, in_specs=in_specs, out_specs=out_specs, check_vma=False)
```

```python
import jax
import jax.numpy as jnp
from jax import lax
from jax.sharding import PartitionSpec as P

BLOCK = 64


adapter_scale = 0.5


def scatter_sum(x, axis):
    count = lax.axis_size(axis)
    pieces = x.astype(jnp.bfloat16).reshape((count, x.shape[0] // count) + x.shape[1:])
    got = lax.all_to_all(pieces, axis, 0, 0, tiled=False)
    return got.astype(jnp.float32).sum(0)


def gather_rows(x, axis):
    count = lax.axis_size(axis)
    got = lax.all_to_all(jnp.broadcast_to(x[None], (count,) + x.shape), axis, 0, 0, tiled=False)
    return got.reshape((count * x.shape[0],) + x.shape[1:])


def shards(
    tokens,
    cotangent,
    gate_weight,
    up_weight,
    down_weight,
    gate_in,
    up_in,
    down_out,
    gate_out,
    up_out,
    down_in,
    tenants,
    owners,
):
    highest = lax.Precision.HIGHEST
    dp_count = lax.axis_size("dp")
    tensor_count = lax.axis_size("tensor")
    dp_index = lax.axis_index("dp")
    tensor_index = lax.axis_index("tensor")
    rows_in = tokens.shape[0]
    feat_here = tokens.shape[1]
    width_here = gate_weight.shape[1]
    rank_width = gate_in.shape[2]
    every_token_row = rows_in * tensor_count
    group_rows = every_token_row // dp_count
    blocks_all = tenants.shape[0]
    blocks_group = group_rows // BLOCK
    blocks_in = rows_in // BLOCK
    tenant_count = owners.shape[0]
    slots_here = tenant_count // dp_count
    tenants_here = tenant_count // tensor_count
    group_tenants = lax.dynamic_slice_in_dim(tenants, dp_index * blocks_group, blocks_group)
    input_tenants = lax.dynamic_slice_in_dim(tenants, tensor_index * blocks_in, blocks_in)
    contract_rows = (((0,), (0,)), ((), ()))
    token_tenants = jnp.broadcast_to(tenants[:, None], (blocks_all, BLOCK)).reshape(every_token_row)
    held_tenants = tensor_index * tenants_here + jnp.arange(tenants_here, dtype=jnp.int32)
    token_onehot = (token_tenants[:, None] == held_tenants[None, :]).astype(jnp.bfloat16)
    all_inputs = lax.all_gather(tokens, "tensor", axis=0, tiled=True)
    cotangent = lax.optimization_barrier((all_inputs, cotangent))[1]
    all_cot = lax.all_gather(cotangent, "tensor", axis=0, tiled=True)

    gate_part = jnp.dot(all_inputs, gate_weight, preferred_element_type=jnp.float32)
    up_part = jnp.dot(all_inputs, up_weight, preferred_element_type=jnp.float32)
    input_blocks = all_inputs.reshape(blocks_all, BLOCK, feat_here)
    gate_rank_part = jnp.einsum(
        "btk,bkr->btr", input_blocks, gate_in[tenants], preferred_element_type=jnp.float32
    ).reshape(every_token_row, rank_width)
    up_rank_part = jnp.einsum(
        "btk,bkr->btr", input_blocks, up_in[tenants], preferred_element_type=jnp.float32
    ).reshape(every_token_row, rank_width)
    forward_sums = scatter_sum(
        jnp.concatenate(
            [
                gate_part.astype(jnp.bfloat16),
                up_part.astype(jnp.bfloat16),
                gate_rank_part.astype(jnp.bfloat16),
                up_rank_part.astype(jnp.bfloat16),
            ],
            axis=1,
        ),
        "dp",
    )
    gate_total_sum = forward_sums[:, :width_here]
    up_total_sum = forward_sums[:, width_here : 2 * width_here]
    gate_rank = forward_sums[:, 2 * width_here : 2 * width_here + rank_width]
    up_rank = forward_sums[:, 2 * width_here + rank_width :]
    gate_rank_second = gate_rank.astype(jnp.bfloat16).reshape(blocks_group, BLOCK, rank_width)
    up_rank_second = up_rank.astype(jnp.bfloat16).reshape(blocks_group, BLOCK, rank_width)
    gate_raise = gate_out[group_tenants]
    up_raise = up_out[group_tenants]
    gate_complete = gate_total_sum + adapter_scale * jnp.einsum(
        "uim,umn->uin", gate_rank_second, gate_raise, preferred_element_type=jnp.float32
    ).reshape(group_rows, width_here)
    up_complete = up_total_sum + adapter_scale * jnp.einsum(
        "uim,umn->uin", up_rank_second, up_raise, preferred_element_type=jnp.float32
    ).reshape(group_rows, width_here)
    hidden = (jax.nn.silu(gate_complete) * up_complete).astype(jnp.bfloat16)
    all_hidden = gather_rows(hidden, "dp")

    hidden_grad_part = lax.dot_general(
        all_cot, down_weight, (((1,), (1,)), ((), ())), preferred_element_type=jnp.float32
    )
    down_back_part = adapter_scale * jnp.einsum(
        "env,ejv->enj",
        all_cot.reshape(blocks_all, BLOCK, feat_here),
        down_out[tenants],
        preferred_element_type=jnp.float32,
    ).reshape(every_token_row, rank_width)
    back_pieces = jnp.concatenate(
        [hidden_grad_part.astype(jnp.bfloat16), down_back_part.astype(jnp.bfloat16)], axis=1
    )
    forward_sums, back_pieces = lax.optimization_barrier((forward_sums, back_pieces))
    back_sums = scatter_sum(back_pieces, "dp")
    hidden_grad_sum = back_sums[:, :width_here]
    group_down_back = back_sums[:, width_here:].astype(jnp.bfloat16)
    down_drop = down_in[group_tenants]
    hidden_grad = hidden_grad_sum + jnp.einsum(
        "btr,bfr->btf",
        group_down_back.reshape(blocks_group, BLOCK, rank_width),
        down_drop,
        preferred_element_type=jnp.float32,
    ).reshape(group_rows, width_here)
    sig = jax.nn.sigmoid(gate_complete)
    up_gradient = (
        (hidden_grad * gate_complete * sig)
        .astype(jnp.bfloat16)
        .reshape(blocks_group, BLOCK, width_here)
    )
    gate_gradient = (
        (hidden_grad * up_complete * sig * (1.0 + gate_complete * (1.0 - sig)))
        .astype(jnp.bfloat16)
        .reshape(blocks_group, BLOCK, width_here)
    )
    gate_backward_piece = adapter_scale * jnp.einsum(
        "yae,yve->yav", gate_gradient, gate_raise, preferred_element_type=jnp.float32
    )
    up_backward_piece = adapter_scale * jnp.einsum(
        "yae,yve->yav", up_gradient, up_raise, preferred_element_type=jnp.float32
    )

    out_part = jnp.dot(all_hidden, down_weight, preferred_element_type=jnp.float32)
    down_rank_part = jnp.einsum(
        "btf,bfr->btr",
        all_hidden.reshape(blocks_all, BLOCK, width_here),
        down_in[tenants],
        preferred_element_type=jnp.float32,
    ).reshape(every_token_row, rank_width)
    rank_back_pieces = jnp.concatenate(
        [
            gate_backward_piece.reshape(group_rows, rank_width),
            up_backward_piece.reshape(group_rows, rank_width),
        ],
        axis=1,
    ).astype(jnp.bfloat16)
    down_pieces = jnp.concatenate(
        [out_part.astype(jnp.bfloat16), down_rank_part.astype(jnp.bfloat16)], axis=1
    ).reshape(tensor_count, rows_in, feat_here + rank_width)
    down_pieces = jnp.concatenate(
        [
            down_pieces,
            jnp.broadcast_to(rank_back_pieces[None], (tensor_count, group_rows, 2 * rank_width)),
        ],
        axis=2,
    )
    down_sums = scatter_sum(down_pieces.reshape(tensor_count * rows_in, -1), "tensor")
    out_sum = down_sums[:, :feat_here]
    down_rank_flat = down_sums[:, feat_here : feat_here + rank_width].astype(jnp.bfloat16)
    gate_backward = down_sums[:, feat_here + rank_width : feat_here + 2 * rank_width]
    up_backward = down_sums[:, feat_here + 2 * rank_width :]
    down_rank_second = down_rank_flat.reshape(blocks_in, BLOCK, rank_width)
    down_raise = down_out[input_tenants]
    mixed = (
        out_sum
        + adapter_scale
        * jnp.einsum(
            "vmn,vnx->vmx", down_rank_second, down_raise, preferred_element_type=jnp.float32
        ).reshape(rows_in, feat_here)
    ).astype(jnp.bfloat16)

    all_down_rank = lax.all_gather(down_rank_flat, "tensor", axis=0, tiled=True)
    rank_weighted = (token_onehot[:, :, None] * all_down_rank[:, None, :]).reshape(
        every_token_row, tenants_here * rank_width
    )
    grad_down_out = adapter_scale * (
        lax.dot_general(rank_weighted, all_cot, contract_rows, preferred_element_type=jnp.float32)
        .reshape(tenants_here, rank_width, feat_here)
    )

    gate_raise_block_list = adapter_scale * jnp.einsum(
        "yap,yau->ypu", gate_rank_second, gate_gradient, preferred_element_type=jnp.float32
    )
    up_raise_block_list = adapter_scale * jnp.einsum(
        "yap,yau->ypu", up_rank_second, up_gradient, preferred_element_type=jnp.float32
    )
    raise_stack = jnp.stack([gate_raise_block_list, up_raise_block_list], axis=1).astype(
        jnp.bfloat16
    )
    backs = jnp.concatenate(
        [gate_backward.astype(jnp.bfloat16), up_backward.astype(jnp.bfloat16), group_down_back],
        axis=1,
    )
    all_joined = gather_rows(
        jnp.concatenate([raise_stack.reshape(-1), backs.reshape(-1)])[None], "dp"
    )
    all_raise_blocks = (
        all_joined[:, : raise_stack.size]
        .reshape((dp_count * blocks_group,) + raise_stack.shape[1:])
        .astype(jnp.float32)
    )
    all_backs = all_joined[:, raise_stack.size :].reshape(every_token_row, 3 * rank_width)
    own_slots = dp_index * slots_here + jnp.arange(slots_here, dtype=jnp.int32)
    block_onehot = (own_slots[:, None] == owners[tenants][None, :]).astype(jnp.float32)
    grad_gate_out = jnp.einsum(
        "sb,brf->srf", block_onehot, all_raise_blocks[:, 0], precision=highest
    )
    grad_up_out = jnp.einsum("sb,brf->srf", block_onehot, all_raise_blocks[:, 1], precision=highest)

    all_gate_back = all_backs[:, :rank_width]
    all_up_back = all_backs[:, rank_width : 2 * rank_width]
    all_down_back = all_backs[:, 2 * rank_width :]
    gate_weighted = (token_onehot[:, :, None] * all_gate_back[:, None, :]).reshape(
        every_token_row, tenants_here * rank_width
    )
    up_weighted = (token_onehot[:, :, None] * all_up_back[:, None, :]).reshape(
        every_token_row, tenants_here * rank_width
    )
    grad_gate_in = (
        lax.dot_general(
            all_inputs, gate_weighted, contract_rows, preferred_element_type=jnp.float32
        )
        .reshape(feat_here, tenants_here, rank_width)
        .transpose(1, 0, 2)
    )
    grad_up_in = (
        lax.dot_general(all_inputs, up_weighted, contract_rows, preferred_element_type=jnp.float32)
        .reshape(feat_here, tenants_here, rank_width)
        .transpose(1, 0, 2)
    )
    block_slot_onehot = (owners[tenants][:, None] == own_slots[None, :]).astype(jnp.bfloat16)
    slot_onehot = jnp.broadcast_to(
        block_slot_onehot[:, None, :], (blocks_all, BLOCK, slots_here)
    ).reshape(every_token_row, slots_here)
    drop_weighted = (slot_onehot[:, :, None] * all_down_back[:, None, :]).reshape(
        every_token_row, slots_here * rank_width
    )
    grad_down_in = (
        lax.dot_general(
            all_hidden, drop_weighted, contract_rows, preferred_element_type=jnp.float32
        )
        .reshape(width_here, slots_here, rank_width)
        .transpose(1, 0, 2)
    )
    return (
        mixed,
        grad_gate_in,
        grad_up_in,
        grad_down_out,
        grad_gate_out,
        grad_up_out,
        grad_down_in,
    )


def solution(mesh):
    in_specs = (
        P("tensor", "dp"),
        P("tensor", "dp"),
        P("dp", "tensor"),
        P("dp", "tensor"),
        P("tensor", "dp"),
        P(None, "dp", None),
        P(None, "dp", None),
        P(None, None, "dp"),
        P(None, None, "tensor"),
        P(None, None, "tensor"),
        P(None, "tensor", None),
        P(),
        P(),
    )
    out_specs = (
        P("tensor", "dp"),
        P("tensor", "dp", None),
        P("tensor", "dp", None),
        P("tensor", None, "dp"),
        P("dp", None, "tensor"),
        P("dp", None, "tensor"),
        P("dp", "tensor", None),
    )
    return jax.shard_map(shards, mesh=mesh, in_specs=in_specs, out_specs=out_specs, check_vma=False)
```

```python
import jax
import jax.numpy as jnp
from jax import lax
from jax.sharding import PartitionSpec as P

BLOCK = 64


adapter_scale = 0.5


def scatter_sum(x, axis):
    count = lax.axis_size(axis)
    pieces = x.astype(jnp.bfloat16).reshape((count, x.shape[0] // count) + x.shape[1:])
    got = lax.all_to_all(pieces, axis, 0, 0, tiled=False)
    return got.astype(jnp.float32).sum(0)


def gather_rows(x, axis):
    count = lax.axis_size(axis)
    got = lax.all_to_all(jnp.broadcast_to(x[None], (count,) + x.shape), axis, 0, 0, tiled=False)
    return got.reshape((count * x.shape[0],) + x.shape[1:])


def shards(
    tokens,
    cotangent,
    gate_weight,
    up_weight,
    down_weight,
    gate_in,
    up_in,
    down_out,
    gate_out,
    up_out,
    down_in,
    tenants,
    owners,
):
    highest = lax.Precision.HIGHEST
    dp_count = lax.axis_size("dp")
    tensor_count = lax.axis_size("tensor")
    dp_index = lax.axis_index("dp")
    tensor_index = lax.axis_index("tensor")
    rows_in = tokens.shape[0]
    feat_here = tokens.shape[1]
    width_here = gate_weight.shape[1]
    rank_width = gate_in.shape[2]
    every_token_row = rows_in * tensor_count
    group_rows = every_token_row // dp_count
    blocks_all = tenants.shape[0]
    blocks_group = group_rows // BLOCK
    blocks_in = rows_in // BLOCK
    tenant_count = owners.shape[0]
    slots_here = tenant_count // dp_count
    tenants_here = tenant_count // tensor_count
    group_tenants = lax.dynamic_slice_in_dim(tenants, dp_index * blocks_group, blocks_group)
    input_tenants = lax.dynamic_slice_in_dim(tenants, tensor_index * blocks_in, blocks_in)
    contract_rows = (((0,), (0,)), ((), ()))
    token_tenants = jnp.broadcast_to(tenants[:, None], (blocks_all, BLOCK)).reshape(every_token_row)
    held_tenants = tensor_index * tenants_here + jnp.arange(tenants_here, dtype=jnp.int32)
    token_onehot = (token_tenants[:, None] == held_tenants[None, :]).astype(jnp.bfloat16)
    all_inputs = lax.all_gather(tokens, "tensor", axis=0, tiled=True)
    cotangent = lax.optimization_barrier((all_inputs, cotangent))[1]
    all_cot = lax.all_gather(cotangent, "tensor", axis=0, tiled=True)

    gate_part = jnp.dot(all_inputs, gate_weight, preferred_element_type=jnp.float32)
    up_part = jnp.dot(all_inputs, up_weight, preferred_element_type=jnp.float32)
    input_blocks = all_inputs.reshape(blocks_all, BLOCK, feat_here)
    gate_rank_part = jnp.einsum(
        "btk,bkr->btr", input_blocks, gate_in[tenants], preferred_element_type=jnp.float32
    ).reshape(every_token_row, rank_width)
    up_rank_part = jnp.einsum(
        "btk,bkr->btr", input_blocks, up_in[tenants], preferred_element_type=jnp.float32
    ).reshape(every_token_row, rank_width)
    forward_sums = scatter_sum(
        jnp.concatenate(
            [
                gate_part.astype(jnp.bfloat16),
                up_part.astype(jnp.bfloat16),
                gate_rank_part.astype(jnp.bfloat16),
                up_rank_part.astype(jnp.bfloat16),
            ],
            axis=1,
        ),
        "dp",
    )
    gate_total_sum = forward_sums[:, :width_here]
    up_total_sum = forward_sums[:, width_here : 2 * width_here]
    gate_rank = forward_sums[:, 2 * width_here : 2 * width_here + rank_width]
    up_rank = forward_sums[:, 2 * width_here + rank_width :]
    gate_rank_second = gate_rank.astype(jnp.bfloat16).reshape(blocks_group, BLOCK, rank_width)
    up_rank_second = up_rank.astype(jnp.bfloat16).reshape(blocks_group, BLOCK, rank_width)
    gate_raise = gate_out[group_tenants]
    up_raise = up_out[group_tenants]
    gate_complete = gate_total_sum + adapter_scale * jnp.einsum(
        "uim,umn->uin", gate_rank_second, gate_raise, preferred_element_type=jnp.float32
    ).reshape(group_rows, width_here)
    up_complete = up_total_sum + adapter_scale * jnp.einsum(
        "uim,umn->uin", up_rank_second, up_raise, preferred_element_type=jnp.float32
    ).reshape(group_rows, width_here)
    hidden = (jax.nn.silu(gate_complete) * up_complete).astype(jnp.bfloat16)
    all_hidden = gather_rows(hidden, "dp")

    hidden_grad_part = lax.dot_general(
        all_cot, down_weight, (((1,), (1,)), ((), ())), preferred_element_type=jnp.float32
    )
    down_back_part = adapter_scale * jnp.einsum(
        "env,ejv->enj",
        all_cot.reshape(blocks_all, BLOCK, feat_here),
        down_out[tenants],
        preferred_element_type=jnp.float32,
    ).reshape(every_token_row, rank_width)
    back_pieces = jnp.concatenate(
        [hidden_grad_part.astype(jnp.bfloat16), down_back_part.astype(jnp.bfloat16)], axis=1
    )
    forward_sums, back_pieces = lax.optimization_barrier((forward_sums, back_pieces))
    back_sums = scatter_sum(back_pieces, "dp")
    hidden_grad_sum = back_sums[:, :width_here]
    group_down_back = back_sums[:, width_here:].astype(jnp.bfloat16)
    down_drop = down_in[group_tenants]
    hidden_grad = hidden_grad_sum + jnp.einsum(
        "btr,bfr->btf",
        group_down_back.reshape(blocks_group, BLOCK, rank_width),
        down_drop,
        preferred_element_type=jnp.float32,
    ).reshape(group_rows, width_here)
    sig = jax.nn.sigmoid(gate_complete)
    up_gradient = (
        (hidden_grad * gate_complete * sig)
        .astype(jnp.bfloat16)
        .reshape(blocks_group, BLOCK, width_here)
    )
    gate_gradient = (
        (hidden_grad * up_complete * sig * (1.0 + gate_complete * (1.0 - sig)))
        .astype(jnp.bfloat16)
        .reshape(blocks_group, BLOCK, width_here)
    )
    gate_backward_piece = adapter_scale * jnp.einsum(
        "yae,yve->yav", gate_gradient, gate_raise, preferred_element_type=jnp.float32
    )
    up_backward_piece = adapter_scale * jnp.einsum(
        "yae,yve->yav", up_gradient, up_raise, preferred_element_type=jnp.float32
    )

    out_part = jnp.dot(all_hidden, down_weight, preferred_element_type=jnp.float32)
    down_rank_part = jnp.einsum(
        "btf,bfr->btr",
        all_hidden.reshape(blocks_all, BLOCK, width_here),
        down_in[tenants],
        preferred_element_type=jnp.float32,
    ).reshape(every_token_row, rank_width)
    rank_back_pieces = jnp.concatenate(
        [
            gate_backward_piece.reshape(group_rows, rank_width),
            up_backward_piece.reshape(group_rows, rank_width),
        ],
        axis=1,
    ).astype(jnp.bfloat16)
    down_pieces = jnp.concatenate(
        [out_part.astype(jnp.bfloat16), down_rank_part.astype(jnp.bfloat16)], axis=1
    ).reshape(tensor_count, rows_in, feat_here + rank_width)
    down_pieces = jnp.concatenate(
        [
            down_pieces,
            jnp.broadcast_to(rank_back_pieces[None], (tensor_count, group_rows, 2 * rank_width)),
        ],
        axis=2,
    )
    down_sums = scatter_sum(down_pieces.reshape(tensor_count * rows_in, -1), "tensor")
    out_sum = down_sums[:, :feat_here]
    down_rank_flat = down_sums[:, feat_here : feat_here + rank_width].astype(jnp.bfloat16)
    gate_backward = down_sums[:, feat_here + rank_width : feat_here + 2 * rank_width]
    up_backward = down_sums[:, feat_here + 2 * rank_width :]
    down_rank_second = down_rank_flat.reshape(blocks_in, BLOCK, rank_width)
    down_raise = down_out[input_tenants]
    mixed = (
        out_sum
        + adapter_scale
        * jnp.einsum(
            "vmn,vnx->vmx", down_rank_second, down_raise, preferred_element_type=jnp.float32
        ).reshape(rows_in, feat_here)
    ).astype(jnp.bfloat16)

    all_down_rank = lax.all_gather(down_rank_flat, "tensor", axis=0, tiled=True)
    rank_weighted = (token_onehot[:, :, None] * all_down_rank[:, None, :]).reshape(
        every_token_row, tenants_here * rank_width
    )
    grad_down_out = adapter_scale * (
        lax.dot_general(rank_weighted, all_cot, contract_rows, preferred_element_type=jnp.float32)
        .reshape(tenants_here, rank_width, feat_here)
    )

    gate_raise_block_list = adapter_scale * jnp.einsum(
        "yap,yau->ypu", gate_rank_second, gate_gradient, preferred_element_type=jnp.float32
    )
    up_raise_block_list = adapter_scale * jnp.einsum(
        "yap,yau->ypu", up_rank_second, up_gradient, preferred_element_type=jnp.float32
    )
    raise_stack = jnp.stack([gate_raise_block_list, up_raise_block_list], axis=1).astype(
        jnp.bfloat16
    )
    backs = jnp.concatenate(
        [gate_backward.astype(jnp.bfloat16), up_backward.astype(jnp.bfloat16), group_down_back],
        axis=1,
    )
    raise_rows = raise_stack.reshape(-1, width_here)
    back_rows = -(-backs.size // (8 * width_here)) * 8
    backs_padded = jnp.pad(backs.reshape(-1), (0, back_rows * width_here - backs.size))
    all_joined = gather_rows(
        jnp.concatenate([raise_rows, backs_padded.reshape(back_rows, width_here)], axis=0), "dp"
    ).reshape(dp_count, -1, width_here)
    all_raise_blocks = (
        all_joined[:, : raise_rows.shape[0]]
        .reshape((dp_count * blocks_group,) + raise_stack.shape[1:])
        .astype(jnp.float32)
    )
    all_backs = (
        all_joined[:, raise_rows.shape[0] :]
        .reshape(dp_count, -1)[:, : backs.size]
        .reshape(every_token_row, 3 * rank_width)
    )
    own_slots = dp_index * slots_here + jnp.arange(slots_here, dtype=jnp.int32)
    block_onehot = (own_slots[:, None] == owners[tenants][None, :]).astype(jnp.float32)
    grad_gate_out = jnp.einsum(
        "sb,brf->srf", block_onehot, all_raise_blocks[:, 0], precision=highest
    )
    grad_up_out = jnp.einsum("sb,brf->srf", block_onehot, all_raise_blocks[:, 1], precision=highest)

    all_gate_back = all_backs[:, :rank_width]
    all_up_back = all_backs[:, rank_width : 2 * rank_width]
    all_down_back = all_backs[:, 2 * rank_width :]
    gate_weighted = (token_onehot[:, :, None] * all_gate_back[:, None, :]).reshape(
        every_token_row, tenants_here * rank_width
    )
    up_weighted = (token_onehot[:, :, None] * all_up_back[:, None, :]).reshape(
        every_token_row, tenants_here * rank_width
    )
    grad_gate_in = (
        lax.dot_general(
            all_inputs, gate_weighted, contract_rows, preferred_element_type=jnp.float32
        )
        .reshape(feat_here, tenants_here, rank_width)
        .transpose(1, 0, 2)
    )
    grad_up_in = (
        lax.dot_general(all_inputs, up_weighted, contract_rows, preferred_element_type=jnp.float32)
        .reshape(feat_here, tenants_here, rank_width)
        .transpose(1, 0, 2)
    )
    block_slot_onehot = (owners[tenants][:, None] == own_slots[None, :]).astype(jnp.bfloat16)
    slot_onehot = jnp.broadcast_to(
        block_slot_onehot[:, None, :], (blocks_all, BLOCK, slots_here)
    ).reshape(every_token_row, slots_here)
    drop_weighted = (slot_onehot[:, :, None] * all_down_back[:, None, :]).reshape(
        every_token_row, slots_here * rank_width
    )
    grad_down_in = (
        lax.dot_general(
            all_hidden, drop_weighted, contract_rows, preferred_element_type=jnp.float32
        )
        .reshape(width_here, slots_here, rank_width)
        .transpose(1, 0, 2)
    )
    return (
        mixed,
        grad_gate_in,
        grad_up_in,
        grad_down_out,
        grad_gate_out,
        grad_up_out,
        grad_down_in,
    )


def solution(mesh):
    in_specs = (
        P("tensor", "dp"),
        P("tensor", "dp"),
        P("dp", "tensor"),
        P("dp", "tensor"),
        P("tensor", "dp"),
        P(None, "dp", None),
        P(None, "dp", None),
        P(None, None, "dp"),
        P(None, None, "tensor"),
        P(None, None, "tensor"),
        P(None, "tensor", None),
        P(),
        P(),
    )
    out_specs = (
        P("tensor", "dp"),
        P("tensor", "dp", None),
        P("tensor", "dp", None),
        P("tensor", None, "dp"),
        P("dp", None, "tensor"),
        P("dp", None, "tensor"),
        P("dp", "tensor", None),
    )
    return jax.shard_map(shards, mesh=mesh, in_specs=in_specs, out_specs=out_specs, check_vma=False)
```

```python
import jax
import jax.numpy as jnp
from jax import lax
from jax.sharding import PartitionSpec as P

BLOCK = 64


adapter_scale = 0.5


def exchange_pieces(x, axis):
    count = lax.axis_size(axis)
    pieces = x.astype(jnp.bfloat16).reshape((count, x.shape[0] // count) + x.shape[1:])
    return lax.all_to_all(pieces, axis, 0, 0, tiled=False)


def scatter_sum(x, axis):
    return exchange_pieces(x, axis).astype(jnp.float32).sum(0)


def gather_rows(x, axis):
    count = lax.axis_size(axis)
    got = lax.all_to_all(jnp.broadcast_to(x[None], (count,) + x.shape), axis, 0, 0, tiled=False)
    return got.reshape((count * x.shape[0],) + x.shape[1:])


def shards(
    tokens,
    cotangent,
    gate_weight,
    up_weight,
    down_weight,
    gate_in,
    up_in,
    down_out,
    gate_out,
    up_out,
    down_in,
    tenants,
    owners,
):
    highest = lax.Precision.HIGHEST
    dp_count = lax.axis_size("dp")
    tensor_count = lax.axis_size("tensor")
    dp_index = lax.axis_index("dp")
    tensor_index = lax.axis_index("tensor")
    rows_in = tokens.shape[0]
    feat_here = tokens.shape[1]
    width_here = gate_weight.shape[1]
    rank_width = gate_in.shape[2]
    every_token_row = rows_in * tensor_count
    group_rows = every_token_row // dp_count
    blocks_all = tenants.shape[0]
    blocks_group = group_rows // BLOCK
    blocks_in = rows_in // BLOCK
    tenant_count = owners.shape[0]
    slots_here = tenant_count // dp_count
    tenants_here = tenant_count // tensor_count
    group_tenants = lax.dynamic_slice_in_dim(tenants, dp_index * blocks_group, blocks_group)
    input_tenants = lax.dynamic_slice_in_dim(tenants, tensor_index * blocks_in, blocks_in)
    contract_rows = (((0,), (0,)), ((), ()))
    token_tenants = jnp.broadcast_to(tenants[:, None], (blocks_all, BLOCK)).reshape(every_token_row)
    held_tenants = tensor_index * tenants_here + jnp.arange(tenants_here, dtype=jnp.int32)
    token_onehot = (token_tenants[:, None] == held_tenants[None, :]).astype(jnp.bfloat16)
    all_inputs = lax.all_gather(tokens, "tensor", axis=0, tiled=True)
    cotangent = lax.optimization_barrier((all_inputs, cotangent))[1]
    all_cot = lax.all_gather(cotangent, "tensor", axis=0, tiled=True)

    gate_part = jnp.dot(all_inputs, gate_weight, preferred_element_type=jnp.float32)
    up_part = jnp.dot(all_inputs, up_weight, preferred_element_type=jnp.float32)
    input_blocks = all_inputs.reshape(blocks_all, BLOCK, feat_here)
    gate_rank_part = jnp.einsum(
        "btk,bkr->btr", input_blocks, gate_in[tenants], preferred_element_type=jnp.float32
    ).reshape(every_token_row, rank_width)
    up_rank_part = jnp.einsum(
        "btk,bkr->btr", input_blocks, up_in[tenants], preferred_element_type=jnp.float32
    ).reshape(every_token_row, rank_width)
    forward_got = exchange_pieces(
        jnp.concatenate(
            [
                gate_part.astype(jnp.bfloat16),
                up_part.astype(jnp.bfloat16),
                gate_rank_part.astype(jnp.bfloat16),
                up_rank_part.astype(jnp.bfloat16),
            ],
            axis=1,
        ),
        "dp",
    )
    forward_sums = forward_got.astype(jnp.float32).sum(0)
    gate_total_sum = forward_sums[:, :width_here]
    up_total_sum = forward_sums[:, width_here : 2 * width_here]
    gate_rank = forward_sums[:, 2 * width_here : 2 * width_here + rank_width]
    up_rank = forward_sums[:, 2 * width_here + rank_width :]
    gate_rank_second = gate_rank.astype(jnp.bfloat16).reshape(blocks_group, BLOCK, rank_width)
    up_rank_second = up_rank.astype(jnp.bfloat16).reshape(blocks_group, BLOCK, rank_width)
    gate_raise = gate_out[group_tenants]
    up_raise = up_out[group_tenants]
    gate_complete = gate_total_sum + adapter_scale * jnp.einsum(
        "uim,umn->uin", gate_rank_second, gate_raise, preferred_element_type=jnp.float32
    ).reshape(group_rows, width_here)
    up_complete = up_total_sum + adapter_scale * jnp.einsum(
        "uim,umn->uin", up_rank_second, up_raise, preferred_element_type=jnp.float32
    ).reshape(group_rows, width_here)
    hidden = (jax.nn.silu(gate_complete) * up_complete).astype(jnp.bfloat16)
    all_hidden = gather_rows(hidden, "dp")

    hidden_grad_part = lax.dot_general(
        all_cot, down_weight, (((1,), (1,)), ((), ())), preferred_element_type=jnp.float32
    )
    down_back_part = adapter_scale * jnp.einsum(
        "env,ejv->enj",
        all_cot.reshape(blocks_all, BLOCK, feat_here),
        down_out[tenants],
        preferred_element_type=jnp.float32,
    ).reshape(every_token_row, rank_width)
    back_pieces = jnp.concatenate(
        [hidden_grad_part.astype(jnp.bfloat16), down_back_part.astype(jnp.bfloat16)], axis=1
    )
    forward_got, back_pieces = lax.optimization_barrier((forward_got, back_pieces))
    back_sums = scatter_sum(back_pieces, "dp")
    hidden_grad_sum = back_sums[:, :width_here]
    group_down_back = back_sums[:, width_here:].astype(jnp.bfloat16)
    down_drop = down_in[group_tenants]
    hidden_grad = hidden_grad_sum + jnp.einsum(
        "btr,bfr->btf",
        group_down_back.reshape(blocks_group, BLOCK, rank_width),
        down_drop,
        preferred_element_type=jnp.float32,
    ).reshape(group_rows, width_here)
    sig = jax.nn.sigmoid(gate_complete)
    up_gradient = (
        (hidden_grad * gate_complete * sig)
        .astype(jnp.bfloat16)
        .reshape(blocks_group, BLOCK, width_here)
    )
    gate_gradient = (
        (hidden_grad * up_complete * sig * (1.0 + gate_complete * (1.0 - sig)))
        .astype(jnp.bfloat16)
        .reshape(blocks_group, BLOCK, width_here)
    )
    gate_backward_piece = adapter_scale * jnp.einsum(
        "yae,yve->yav", gate_gradient, gate_raise, preferred_element_type=jnp.float32
    )
    up_backward_piece = adapter_scale * jnp.einsum(
        "yae,yve->yav", up_gradient, up_raise, preferred_element_type=jnp.float32
    )

    out_part = jnp.dot(all_hidden, down_weight, preferred_element_type=jnp.float32)
    down_rank_part = jnp.einsum(
        "btf,bfr->btr",
        all_hidden.reshape(blocks_all, BLOCK, width_here),
        down_in[tenants],
        preferred_element_type=jnp.float32,
    ).reshape(every_token_row, rank_width)
    rank_back_pieces = jnp.concatenate(
        [
            gate_backward_piece.reshape(group_rows, rank_width),
            up_backward_piece.reshape(group_rows, rank_width),
        ],
        axis=1,
    ).astype(jnp.bfloat16)
    down_pieces = jnp.concatenate(
        [out_part.astype(jnp.bfloat16), down_rank_part.astype(jnp.bfloat16)], axis=1
    ).reshape(tensor_count, rows_in, feat_here + rank_width)
    down_pieces = jnp.concatenate(
        [
            down_pieces,
            jnp.broadcast_to(rank_back_pieces[None], (tensor_count, group_rows, 2 * rank_width)),
        ],
        axis=2,
    )
    down_sums = scatter_sum(down_pieces.reshape(tensor_count * rows_in, -1), "tensor")
    out_sum = down_sums[:, :feat_here]
    down_rank_flat = down_sums[:, feat_here : feat_here + rank_width].astype(jnp.bfloat16)
    gate_backward = down_sums[:, feat_here + rank_width : feat_here + 2 * rank_width]
    up_backward = down_sums[:, feat_here + 2 * rank_width :]
    down_rank_second = down_rank_flat.reshape(blocks_in, BLOCK, rank_width)
    down_raise = down_out[input_tenants]
    mixed = (
        out_sum
        + adapter_scale
        * jnp.einsum(
            "vmn,vnx->vmx", down_rank_second, down_raise, preferred_element_type=jnp.float32
        ).reshape(rows_in, feat_here)
    ).astype(jnp.bfloat16)

    all_down_rank = lax.all_gather(down_rank_flat, "tensor", axis=0, tiled=True)
    rank_weighted = (token_onehot[:, :, None] * all_down_rank[:, None, :]).reshape(
        every_token_row, tenants_here * rank_width
    )
    grad_down_out = adapter_scale * (
        lax.dot_general(rank_weighted, all_cot, contract_rows, preferred_element_type=jnp.float32)
        .reshape(tenants_here, rank_width, feat_here)
    )

    gate_raise_block_list = adapter_scale * jnp.einsum(
        "yap,yau->ypu", gate_rank_second, gate_gradient, preferred_element_type=jnp.float32
    )
    up_raise_block_list = adapter_scale * jnp.einsum(
        "yap,yau->ypu", up_rank_second, up_gradient, preferred_element_type=jnp.float32
    )
    raise_stack = jnp.stack([gate_raise_block_list, up_raise_block_list], axis=1).astype(
        jnp.bfloat16
    )
    backs = jnp.concatenate(
        [gate_backward.astype(jnp.bfloat16), up_backward.astype(jnp.bfloat16), group_down_back],
        axis=1,
    )
    raise_rows = raise_stack.reshape(-1, width_here)
    back_rows = -(-backs.size // (8 * width_here)) * 8
    backs_padded = jnp.pad(backs.reshape(-1), (0, back_rows * width_here - backs.size))
    all_joined = gather_rows(
        jnp.concatenate([raise_rows, backs_padded.reshape(back_rows, width_here)], axis=0), "dp"
    ).reshape(dp_count, -1, width_here)
    all_raise_blocks = (
        all_joined[:, : raise_rows.shape[0]]
        .reshape((dp_count * blocks_group,) + raise_stack.shape[1:])
        .astype(jnp.float32)
    )
    all_backs = (
        all_joined[:, raise_rows.shape[0] :]
        .reshape(dp_count, -1)[:, : backs.size]
        .reshape(every_token_row, 3 * rank_width)
    )
    own_slots = dp_index * slots_here + jnp.arange(slots_here, dtype=jnp.int32)
    block_onehot = (own_slots[:, None] == owners[tenants][None, :]).astype(jnp.float32)
    grad_gate_out = jnp.einsum(
        "sb,brf->srf", block_onehot, all_raise_blocks[:, 0], precision=highest
    )
    grad_up_out = jnp.einsum("sb,brf->srf", block_onehot, all_raise_blocks[:, 1], precision=highest)

    all_gate_back = all_backs[:, :rank_width]
    all_up_back = all_backs[:, rank_width : 2 * rank_width]
    all_down_back = all_backs[:, 2 * rank_width :]
    gate_weighted = (token_onehot[:, :, None] * all_gate_back[:, None, :]).reshape(
        every_token_row, tenants_here * rank_width
    )
    up_weighted = (token_onehot[:, :, None] * all_up_back[:, None, :]).reshape(
        every_token_row, tenants_here * rank_width
    )
    grad_gate_in = (
        lax.dot_general(
            all_inputs, gate_weighted, contract_rows, preferred_element_type=jnp.float32
        )
        .reshape(feat_here, tenants_here, rank_width)
        .transpose(1, 0, 2)
    )
    grad_up_in = (
        lax.dot_general(all_inputs, up_weighted, contract_rows, preferred_element_type=jnp.float32)
        .reshape(feat_here, tenants_here, rank_width)
        .transpose(1, 0, 2)
    )
    block_slot_onehot = (owners[tenants][:, None] == own_slots[None, :]).astype(jnp.bfloat16)
    slot_onehot = jnp.broadcast_to(
        block_slot_onehot[:, None, :], (blocks_all, BLOCK, slots_here)
    ).reshape(every_token_row, slots_here)
    drop_weighted = (slot_onehot[:, :, None] * all_down_back[:, None, :]).reshape(
        every_token_row, slots_here * rank_width
    )
    grad_down_in = (
        lax.dot_general(
            all_hidden, drop_weighted, contract_rows, preferred_element_type=jnp.float32
        )
        .reshape(width_here, slots_here, rank_width)
        .transpose(1, 0, 2)
    )
    return (
        mixed,
        grad_gate_in,
        grad_up_in,
        grad_down_out,
        grad_gate_out,
        grad_up_out,
        grad_down_in,
    )


def solution(mesh):
    in_specs = (
        P("tensor", "dp"),
        P("tensor", "dp"),
        P("dp", "tensor"),
        P("dp", "tensor"),
        P("tensor", "dp"),
        P(None, "dp", None),
        P(None, "dp", None),
        P(None, None, "dp"),
        P(None, None, "tensor"),
        P(None, None, "tensor"),
        P(None, "tensor", None),
        P(),
        P(),
    )
    out_specs = (
        P("tensor", "dp"),
        P("tensor", "dp", None),
        P("tensor", "dp", None),
        P("tensor", None, "dp"),
        P("dp", None, "tensor"),
        P("dp", None, "tensor"),
        P("dp", "tensor", None),
    )
    return jax.shard_map(shards, mesh=mesh, in_specs=in_specs, out_specs=out_specs, check_vma=False)
```

```python
import jax
import jax.numpy as jnp
from jax import lax
from jax.sharding import PartitionSpec as P

BLOCK = 64


adapter_scale = 0.5


def exchange_pieces(x, axis):
    count = lax.axis_size(axis)
    pieces = x.astype(jnp.bfloat16).reshape((count, x.shape[0] // count) + x.shape[1:])
    return lax.all_to_all(pieces, axis, 0, 0, tiled=False)


def scatter_sum(x, axis):
    return exchange_pieces(x, axis).astype(jnp.float32).sum(0)


def gather_rows(x, axis):
    count = lax.axis_size(axis)
    got = lax.all_to_all(jnp.broadcast_to(x[None], (count,) + x.shape), axis, 0, 0, tiled=False)
    return got.reshape((count * x.shape[0],) + x.shape[1:])


def shards(
    tokens,
    cotangent,
    gate_weight,
    up_weight,
    down_weight,
    gate_in,
    up_in,
    down_out,
    gate_out,
    up_out,
    down_in,
    tenants,
    owners,
):
    highest = lax.Precision.HIGHEST
    dp_count = lax.axis_size("dp")
    tensor_count = lax.axis_size("tensor")
    dp_index = lax.axis_index("dp")
    tensor_index = lax.axis_index("tensor")
    rows_in = tokens.shape[0]
    feat_here = tokens.shape[1]
    width_here = gate_weight.shape[1]
    rank_width = gate_in.shape[2]
    every_token_row = rows_in * tensor_count
    group_rows = every_token_row // dp_count
    blocks_all = tenants.shape[0]
    blocks_group = group_rows // BLOCK
    blocks_in = rows_in // BLOCK
    tenant_count = owners.shape[0]
    slots_here = tenant_count // dp_count
    tenants_here = tenant_count // tensor_count
    group_tenants = lax.dynamic_slice_in_dim(tenants, dp_index * blocks_group, blocks_group)
    input_tenants = lax.dynamic_slice_in_dim(tenants, tensor_index * blocks_in, blocks_in)
    contract_rows = (((0,), (0,)), ((), ()))
    token_tenants = jnp.broadcast_to(tenants[:, None], (blocks_all, BLOCK)).reshape(every_token_row)
    held_tenants = tensor_index * tenants_here + jnp.arange(tenants_here, dtype=jnp.int32)
    token_onehot = (token_tenants[:, None] == held_tenants[None, :]).astype(jnp.bfloat16)
    all_inputs = gather_rows(tokens, "tensor")
    cotangent = lax.optimization_barrier((all_inputs, cotangent))[1]
    all_cot = gather_rows(cotangent, "tensor")

    gate_part = jnp.dot(all_inputs, gate_weight, preferred_element_type=jnp.float32)
    up_part = jnp.dot(all_inputs, up_weight, preferred_element_type=jnp.float32)
    input_blocks = all_inputs.reshape(blocks_all, BLOCK, feat_here)
    gate_rank_part = jnp.einsum(
        "btk,bkr->btr", input_blocks, gate_in[tenants], preferred_element_type=jnp.float32
    ).reshape(every_token_row, rank_width)
    up_rank_part = jnp.einsum(
        "btk,bkr->btr", input_blocks, up_in[tenants], preferred_element_type=jnp.float32
    ).reshape(every_token_row, rank_width)
    forward_got = exchange_pieces(
        jnp.concatenate(
            [
                gate_part.astype(jnp.bfloat16),
                up_part.astype(jnp.bfloat16),
                gate_rank_part.astype(jnp.bfloat16),
                up_rank_part.astype(jnp.bfloat16),
            ],
            axis=1,
        ),
        "dp",
    )
    forward_sums = forward_got.astype(jnp.float32).sum(0)
    gate_total_sum = forward_sums[:, :width_here]
    up_total_sum = forward_sums[:, width_here : 2 * width_here]
    gate_rank = forward_sums[:, 2 * width_here : 2 * width_here + rank_width]
    up_rank = forward_sums[:, 2 * width_here + rank_width :]
    gate_rank_second = gate_rank.astype(jnp.bfloat16).reshape(blocks_group, BLOCK, rank_width)
    up_rank_second = up_rank.astype(jnp.bfloat16).reshape(blocks_group, BLOCK, rank_width)
    gate_raise = gate_out[group_tenants]
    up_raise = up_out[group_tenants]
    gate_complete = gate_total_sum + adapter_scale * jnp.einsum(
        "uim,umn->uin", gate_rank_second, gate_raise, preferred_element_type=jnp.float32
    ).reshape(group_rows, width_here)
    up_complete = up_total_sum + adapter_scale * jnp.einsum(
        "uim,umn->uin", up_rank_second, up_raise, preferred_element_type=jnp.float32
    ).reshape(group_rows, width_here)
    hidden = (jax.nn.silu(gate_complete) * up_complete).astype(jnp.bfloat16)
    all_hidden = gather_rows(hidden, "dp")

    hidden_grad_part = lax.dot_general(
        all_cot, down_weight, (((1,), (1,)), ((), ())), preferred_element_type=jnp.float32
    )
    down_back_part = adapter_scale * jnp.einsum(
        "env,ejv->enj",
        all_cot.reshape(blocks_all, BLOCK, feat_here),
        down_out[tenants],
        preferred_element_type=jnp.float32,
    ).reshape(every_token_row, rank_width)
    back_pieces = jnp.concatenate(
        [hidden_grad_part.astype(jnp.bfloat16), down_back_part.astype(jnp.bfloat16)], axis=1
    )
    forward_got, back_pieces = lax.optimization_barrier((forward_got, back_pieces))
    back_sums = scatter_sum(back_pieces, "dp")
    hidden_grad_sum = back_sums[:, :width_here]
    group_down_back = back_sums[:, width_here:].astype(jnp.bfloat16)
    down_drop = down_in[group_tenants]
    hidden_grad = hidden_grad_sum + jnp.einsum(
        "btr,bfr->btf",
        group_down_back.reshape(blocks_group, BLOCK, rank_width),
        down_drop,
        preferred_element_type=jnp.float32,
    ).reshape(group_rows, width_here)
    sig = jax.nn.sigmoid(gate_complete)
    up_gradient = (
        (hidden_grad * gate_complete * sig)
        .astype(jnp.bfloat16)
        .reshape(blocks_group, BLOCK, width_here)
    )
    gate_gradient = (
        (hidden_grad * up_complete * sig * (1.0 + gate_complete * (1.0 - sig)))
        .astype(jnp.bfloat16)
        .reshape(blocks_group, BLOCK, width_here)
    )
    gate_backward_piece = adapter_scale * jnp.einsum(
        "yae,yve->yav", gate_gradient, gate_raise, preferred_element_type=jnp.float32
    )
    up_backward_piece = adapter_scale * jnp.einsum(
        "yae,yve->yav", up_gradient, up_raise, preferred_element_type=jnp.float32
    )

    out_part = jnp.dot(all_hidden, down_weight, preferred_element_type=jnp.float32)
    down_rank_part = jnp.einsum(
        "btf,bfr->btr",
        all_hidden.reshape(blocks_all, BLOCK, width_here),
        down_in[tenants],
        preferred_element_type=jnp.float32,
    ).reshape(every_token_row, rank_width)
    rank_back_pieces = jnp.concatenate(
        [
            gate_backward_piece.reshape(group_rows, rank_width),
            up_backward_piece.reshape(group_rows, rank_width),
        ],
        axis=1,
    ).astype(jnp.bfloat16)
    down_pieces = jnp.concatenate(
        [out_part.astype(jnp.bfloat16), down_rank_part.astype(jnp.bfloat16)], axis=1
    ).reshape(tensor_count, rows_in, feat_here + rank_width)
    down_pieces = jnp.concatenate(
        [
            down_pieces,
            jnp.broadcast_to(rank_back_pieces[None], (tensor_count, group_rows, 2 * rank_width)),
        ],
        axis=2,
    )
    down_sums = scatter_sum(down_pieces.reshape(tensor_count * rows_in, -1), "tensor")
    out_sum = down_sums[:, :feat_here]
    down_rank_flat = down_sums[:, feat_here : feat_here + rank_width].astype(jnp.bfloat16)
    gate_backward = down_sums[:, feat_here + rank_width : feat_here + 2 * rank_width]
    up_backward = down_sums[:, feat_here + 2 * rank_width :]
    down_rank_second = down_rank_flat.reshape(blocks_in, BLOCK, rank_width)
    down_raise = down_out[input_tenants]
    mixed = (
        out_sum
        + adapter_scale
        * jnp.einsum(
            "vmn,vnx->vmx", down_rank_second, down_raise, preferred_element_type=jnp.float32
        ).reshape(rows_in, feat_here)
    ).astype(jnp.bfloat16)

    all_down_rank = lax.all_gather(down_rank_flat, "tensor", axis=0, tiled=True)
    rank_weighted = (token_onehot[:, :, None] * all_down_rank[:, None, :]).reshape(
        every_token_row, tenants_here * rank_width
    )
    grad_down_out = adapter_scale * (
        lax.dot_general(rank_weighted, all_cot, contract_rows, preferred_element_type=jnp.float32)
        .reshape(tenants_here, rank_width, feat_here)
    )

    gate_raise_block_list = adapter_scale * jnp.einsum(
        "yap,yau->ypu", gate_rank_second, gate_gradient, preferred_element_type=jnp.float32
    )
    up_raise_block_list = adapter_scale * jnp.einsum(
        "yap,yau->ypu", up_rank_second, up_gradient, preferred_element_type=jnp.float32
    )
    raise_stack = jnp.stack([gate_raise_block_list, up_raise_block_list], axis=1).astype(
        jnp.bfloat16
    )
    backs = jnp.concatenate(
        [gate_backward.astype(jnp.bfloat16), up_backward.astype(jnp.bfloat16), group_down_back],
        axis=1,
    )
    raise_rows = raise_stack.reshape(-1, width_here)
    back_rows = -(-backs.size // (8 * width_here)) * 8
    backs_padded = jnp.pad(backs.reshape(-1), (0, back_rows * width_here - backs.size))
    all_joined = gather_rows(
        jnp.concatenate([raise_rows, backs_padded.reshape(back_rows, width_here)], axis=0), "dp"
    ).reshape(dp_count, -1, width_here)
    all_raise_blocks = (
        all_joined[:, : raise_rows.shape[0]]
        .reshape((dp_count * blocks_group,) + raise_stack.shape[1:])
        .astype(jnp.float32)
    )
    all_backs = (
        all_joined[:, raise_rows.shape[0] :]
        .reshape(dp_count, -1)[:, : backs.size]
        .reshape(every_token_row, 3 * rank_width)
    )
    own_slots = dp_index * slots_here + jnp.arange(slots_here, dtype=jnp.int32)
    block_onehot = (own_slots[:, None] == owners[tenants][None, :]).astype(jnp.float32)
    grad_gate_out = jnp.einsum(
        "sb,brf->srf", block_onehot, all_raise_blocks[:, 0], precision=highest
    )
    grad_up_out = jnp.einsum("sb,brf->srf", block_onehot, all_raise_blocks[:, 1], precision=highest)

    all_gate_back = all_backs[:, :rank_width]
    all_up_back = all_backs[:, rank_width : 2 * rank_width]
    all_down_back = all_backs[:, 2 * rank_width :]
    gate_weighted = (token_onehot[:, :, None] * all_gate_back[:, None, :]).reshape(
        every_token_row, tenants_here * rank_width
    )
    up_weighted = (token_onehot[:, :, None] * all_up_back[:, None, :]).reshape(
        every_token_row, tenants_here * rank_width
    )
    grad_gate_in = (
        lax.dot_general(
            all_inputs, gate_weighted, contract_rows, preferred_element_type=jnp.float32
        )
        .reshape(feat_here, tenants_here, rank_width)
        .transpose(1, 0, 2)
    )
    grad_up_in = (
        lax.dot_general(all_inputs, up_weighted, contract_rows, preferred_element_type=jnp.float32)
        .reshape(feat_here, tenants_here, rank_width)
        .transpose(1, 0, 2)
    )
    block_slot_onehot = (owners[tenants][:, None] == own_slots[None, :]).astype(jnp.bfloat16)
    slot_onehot = jnp.broadcast_to(
        block_slot_onehot[:, None, :], (blocks_all, BLOCK, slots_here)
    ).reshape(every_token_row, slots_here)
    drop_weighted = (slot_onehot[:, :, None] * all_down_back[:, None, :]).reshape(
        every_token_row, slots_here * rank_width
    )
    grad_down_in = (
        lax.dot_general(
            all_hidden, drop_weighted, contract_rows, preferred_element_type=jnp.float32
        )
        .reshape(width_here, slots_here, rank_width)
        .transpose(1, 0, 2)
    )
    return (
        mixed,
        grad_gate_in,
        grad_up_in,
        grad_down_out,
        grad_gate_out,
        grad_up_out,
        grad_down_in,
    )


def solution(mesh):
    in_specs = (
        P("tensor", "dp"),
        P("tensor", "dp"),
        P("dp", "tensor"),
        P("dp", "tensor"),
        P("tensor", "dp"),
        P(None, "dp", None),
        P(None, "dp", None),
        P(None, None, "dp"),
        P(None, None, "tensor"),
        P(None, None, "tensor"),
        P(None, "tensor", None),
        P(),
        P(),
    )
    out_specs = (
        P("tensor", "dp"),
        P("tensor", "dp", None),
        P("tensor", "dp", None),
        P("tensor", None, "dp"),
        P("dp", None, "tensor"),
        P("dp", None, "tensor"),
        P("dp", "tensor", None),
    )
    return jax.shard_map(shards, mesh=mesh, in_specs=in_specs, out_specs=out_specs, check_vma=False)
```

```python
import jax
import jax.numpy as jnp
from jax import lax
from jax.sharding import PartitionSpec as P

BLOCK = 64


adapter_scale = 0.5


def exchange_pieces(x, axis):
    count = lax.axis_size(axis)
    pieces = x.astype(jnp.bfloat16).reshape((count, x.shape[0] // count) + x.shape[1:])
    return lax.all_to_all(pieces, axis, 0, 0, tiled=False)


def scatter_sum(x, axis):
    return exchange_pieces(x, axis).astype(jnp.float32).sum(0)


def gather_rows(x, axis):
    count = lax.axis_size(axis)
    got = lax.all_to_all(jnp.broadcast_to(x[None], (count,) + x.shape), axis, 0, 0, tiled=False)
    return got.reshape((count * x.shape[0],) + x.shape[1:])


def shards(
    tokens,
    cotangent,
    gate_weight,
    up_weight,
    down_weight,
    gate_in,
    up_in,
    down_out,
    gate_out,
    up_out,
    down_in,
    tenants,
    owners,
):
    highest = lax.Precision.HIGHEST
    dp_count = lax.axis_size("dp")
    tensor_count = lax.axis_size("tensor")
    dp_index = lax.axis_index("dp")
    tensor_index = lax.axis_index("tensor")
    rows_in = tokens.shape[0]
    feat_here = tokens.shape[1]
    width_here = gate_weight.shape[1]
    rank_width = gate_in.shape[2]
    every_token_row = rows_in * tensor_count
    group_rows = every_token_row // dp_count
    blocks_all = tenants.shape[0]
    blocks_group = group_rows // BLOCK
    blocks_in = rows_in // BLOCK
    tenant_count = owners.shape[0]
    slots_here = tenant_count // dp_count
    tenants_here = tenant_count // tensor_count
    group_tenants = lax.dynamic_slice_in_dim(tenants, dp_index * blocks_group, blocks_group)
    input_tenants = lax.dynamic_slice_in_dim(tenants, tensor_index * blocks_in, blocks_in)
    contract_rows = (((0,), (0,)), ((), ()))
    token_tenants = jnp.broadcast_to(tenants[:, None], (blocks_all, BLOCK)).reshape(every_token_row)
    held_tenants = tensor_index * tenants_here + jnp.arange(tenants_here, dtype=jnp.int32)
    token_onehot = (token_tenants[:, None] == held_tenants[None, :]).astype(jnp.bfloat16)
    all_inputs = lax.all_gather(tokens, "tensor", axis=0, tiled=True)
    cotangent = lax.optimization_barrier((all_inputs, cotangent))[1]
    all_cot = lax.all_gather(cotangent, "tensor", axis=0, tiled=True)

    gate_part = jnp.dot(all_inputs, gate_weight, preferred_element_type=jnp.float32)
    up_part = jnp.dot(all_inputs, up_weight, preferred_element_type=jnp.float32)
    input_blocks = all_inputs.reshape(blocks_all, BLOCK, feat_here)
    gate_rank_part = jnp.einsum(
        "btk,bkr->btr", input_blocks, gate_in[tenants], preferred_element_type=jnp.float32
    ).reshape(every_token_row, rank_width)
    up_rank_part = jnp.einsum(
        "btk,bkr->btr", input_blocks, up_in[tenants], preferred_element_type=jnp.float32
    ).reshape(every_token_row, rank_width)
    forward_got = exchange_pieces(
        jnp.concatenate(
            [
                gate_part.astype(jnp.bfloat16),
                up_part.astype(jnp.bfloat16),
                gate_rank_part.astype(jnp.bfloat16),
                up_rank_part.astype(jnp.bfloat16),
            ],
            axis=1,
        ),
        "dp",
    )
    forward_sums = forward_got.astype(jnp.float32).sum(0)
    gate_total_sum = forward_sums[:, :width_here]
    up_total_sum = forward_sums[:, width_here : 2 * width_here]
    gate_rank = forward_sums[:, 2 * width_here : 2 * width_here + rank_width]
    up_rank = forward_sums[:, 2 * width_here + rank_width :]
    gate_rank_second = gate_rank.astype(jnp.bfloat16).reshape(blocks_group, BLOCK, rank_width)
    up_rank_second = up_rank.astype(jnp.bfloat16).reshape(blocks_group, BLOCK, rank_width)
    gate_raise = gate_out[group_tenants]
    up_raise = up_out[group_tenants]
    gate_complete = gate_total_sum + adapter_scale * jnp.einsum(
        "uim,umn->uin", gate_rank_second, gate_raise, preferred_element_type=jnp.float32
    ).reshape(group_rows, width_here)
    up_complete = up_total_sum + adapter_scale * jnp.einsum(
        "uim,umn->uin", up_rank_second, up_raise, preferred_element_type=jnp.float32
    ).reshape(group_rows, width_here)
    hidden = (jax.nn.silu(gate_complete) * up_complete).astype(jnp.bfloat16)
    all_hidden = gather_rows(hidden, "dp")

    hidden_grad_part = lax.dot_general(
        all_cot, down_weight, (((1,), (1,)), ((), ())), preferred_element_type=jnp.float32
    )
    down_back_part = adapter_scale * jnp.einsum(
        "env,ejv->enj",
        all_cot.reshape(blocks_all, BLOCK, feat_here),
        down_out[tenants],
        preferred_element_type=jnp.float32,
    ).reshape(every_token_row, rank_width)
    back_pieces = jnp.concatenate(
        [hidden_grad_part.astype(jnp.bfloat16), down_back_part.astype(jnp.bfloat16)], axis=1
    )
    all_hidden, back_pieces = lax.optimization_barrier((all_hidden, back_pieces))
    back_sums = scatter_sum(back_pieces, "dp")
    hidden_grad_sum = back_sums[:, :width_here]
    group_down_back = back_sums[:, width_here:].astype(jnp.bfloat16)
    down_drop = down_in[group_tenants]
    hidden_grad = hidden_grad_sum + jnp.einsum(
        "btr,bfr->btf",
        group_down_back.reshape(blocks_group, BLOCK, rank_width),
        down_drop,
        preferred_element_type=jnp.float32,
    ).reshape(group_rows, width_here)
    sig = jax.nn.sigmoid(gate_complete)
    up_gradient = (
        (hidden_grad * gate_complete * sig)
        .astype(jnp.bfloat16)
        .reshape(blocks_group, BLOCK, width_here)
    )
    gate_gradient = (
        (hidden_grad * up_complete * sig * (1.0 + gate_complete * (1.0 - sig)))
        .astype(jnp.bfloat16)
        .reshape(blocks_group, BLOCK, width_here)
    )
    gate_backward_piece = adapter_scale * jnp.einsum(
        "yae,yve->yav", gate_gradient, gate_raise, preferred_element_type=jnp.float32
    )
    up_backward_piece = adapter_scale * jnp.einsum(
        "yae,yve->yav", up_gradient, up_raise, preferred_element_type=jnp.float32
    )

    out_part = jnp.dot(all_hidden, down_weight, preferred_element_type=jnp.float32)
    down_rank_part = jnp.einsum(
        "btf,bfr->btr",
        all_hidden.reshape(blocks_all, BLOCK, width_here),
        down_in[tenants],
        preferred_element_type=jnp.float32,
    ).reshape(every_token_row, rank_width)
    rank_back_pieces = jnp.concatenate(
        [
            gate_backward_piece.reshape(group_rows, rank_width),
            up_backward_piece.reshape(group_rows, rank_width),
        ],
        axis=1,
    ).astype(jnp.bfloat16)
    down_pieces = jnp.concatenate(
        [out_part.astype(jnp.bfloat16), down_rank_part.astype(jnp.bfloat16)], axis=1
    ).reshape(tensor_count, rows_in, feat_here + rank_width)
    down_pieces = jnp.concatenate(
        [
            down_pieces,
            jnp.broadcast_to(rank_back_pieces[None], (tensor_count, group_rows, 2 * rank_width)),
        ],
        axis=2,
    )
    down_sums = scatter_sum(down_pieces.reshape(tensor_count * rows_in, -1), "tensor")
    out_sum = down_sums[:, :feat_here]
    down_rank_flat = down_sums[:, feat_here : feat_here + rank_width].astype(jnp.bfloat16)
    gate_backward = down_sums[:, feat_here + rank_width : feat_here + 2 * rank_width]
    up_backward = down_sums[:, feat_here + 2 * rank_width :]
    down_rank_second = down_rank_flat.reshape(blocks_in, BLOCK, rank_width)
    down_raise = down_out[input_tenants]
    mixed = (
        out_sum
        + adapter_scale
        * jnp.einsum(
            "vmn,vnx->vmx", down_rank_second, down_raise, preferred_element_type=jnp.float32
        ).reshape(rows_in, feat_here)
    ).astype(jnp.bfloat16)

    all_down_rank = lax.all_gather(down_rank_flat, "tensor", axis=0, tiled=True)
    rank_weighted = (token_onehot[:, :, None] * all_down_rank[:, None, :]).reshape(
        every_token_row, tenants_here * rank_width
    )
    grad_down_out = adapter_scale * (
        lax.dot_general(rank_weighted, all_cot, contract_rows, preferred_element_type=jnp.float32)
        .reshape(tenants_here, rank_width, feat_here)
    )

    gate_raise_block_list = adapter_scale * jnp.einsum(
        "yap,yau->ypu", gate_rank_second, gate_gradient, preferred_element_type=jnp.float32
    )
    up_raise_block_list = adapter_scale * jnp.einsum(
        "yap,yau->ypu", up_rank_second, up_gradient, preferred_element_type=jnp.float32
    )
    raise_stack = jnp.stack([gate_raise_block_list, up_raise_block_list], axis=1).astype(
        jnp.bfloat16
    )
    backs = jnp.concatenate(
        [gate_backward.astype(jnp.bfloat16), up_backward.astype(jnp.bfloat16), group_down_back],
        axis=1,
    )
    raise_rows = raise_stack.reshape(-1, width_here)
    back_rows = -(-backs.size // (8 * width_here)) * 8
    backs_padded = jnp.pad(backs.reshape(-1), (0, back_rows * width_here - backs.size))
    all_joined = gather_rows(
        jnp.concatenate([raise_rows, backs_padded.reshape(back_rows, width_here)], axis=0), "dp"
    ).reshape(dp_count, -1, width_here)
    all_raise_blocks = (
        all_joined[:, : raise_rows.shape[0]]
        .reshape((dp_count * blocks_group,) + raise_stack.shape[1:])
        .astype(jnp.float32)
    )
    all_backs = (
        all_joined[:, raise_rows.shape[0] :]
        .reshape(dp_count, -1)[:, : backs.size]
        .reshape(every_token_row, 3 * rank_width)
    )
    own_slots = dp_index * slots_here + jnp.arange(slots_here, dtype=jnp.int32)
    block_onehot = (own_slots[:, None] == owners[tenants][None, :]).astype(jnp.float32)
    grad_gate_out = jnp.einsum(
        "sb,brf->srf", block_onehot, all_raise_blocks[:, 0], precision=highest
    )
    grad_up_out = jnp.einsum("sb,brf->srf", block_onehot, all_raise_blocks[:, 1], precision=highest)

    all_gate_back = all_backs[:, :rank_width]
    all_up_back = all_backs[:, rank_width : 2 * rank_width]
    all_down_back = all_backs[:, 2 * rank_width :]
    gate_weighted = (token_onehot[:, :, None] * all_gate_back[:, None, :]).reshape(
        every_token_row, tenants_here * rank_width
    )
    up_weighted = (token_onehot[:, :, None] * all_up_back[:, None, :]).reshape(
        every_token_row, tenants_here * rank_width
    )
    grad_gate_in = (
        lax.dot_general(
            all_inputs, gate_weighted, contract_rows, preferred_element_type=jnp.float32
        )
        .reshape(feat_here, tenants_here, rank_width)
        .transpose(1, 0, 2)
    )
    grad_up_in = (
        lax.dot_general(all_inputs, up_weighted, contract_rows, preferred_element_type=jnp.float32)
        .reshape(feat_here, tenants_here, rank_width)
        .transpose(1, 0, 2)
    )
    block_slot_onehot = (owners[tenants][:, None] == own_slots[None, :]).astype(jnp.bfloat16)
    slot_onehot = jnp.broadcast_to(
        block_slot_onehot[:, None, :], (blocks_all, BLOCK, slots_here)
    ).reshape(every_token_row, slots_here)
    drop_weighted = (slot_onehot[:, :, None] * all_down_back[:, None, :]).reshape(
        every_token_row, slots_here * rank_width
    )
    grad_down_in = (
        lax.dot_general(
            all_hidden, drop_weighted, contract_rows, preferred_element_type=jnp.float32
        )
        .reshape(width_here, slots_here, rank_width)
        .transpose(1, 0, 2)
    )
    return (
        mixed,
        grad_gate_in,
        grad_up_in,
        grad_down_out,
        grad_gate_out,
        grad_up_out,
        grad_down_in,
    )


def solution(mesh):
    in_specs = (
        P("tensor", "dp"),
        P("tensor", "dp"),
        P("dp", "tensor"),
        P("dp", "tensor"),
        P("tensor", "dp"),
        P(None, "dp", None),
        P(None, "dp", None),
        P(None, None, "dp"),
        P(None, None, "tensor"),
        P(None, None, "tensor"),
        P(None, "tensor", None),
        P(),
        P(),
    )
    out_specs = (
        P("tensor", "dp"),
        P("tensor", "dp", None),
        P("tensor", "dp", None),
        P("tensor", None, "dp"),
        P("dp", None, "tensor"),
        P("dp", None, "tensor"),
        P("dp", "tensor", None),
    )
    return jax.shard_map(shards, mesh=mesh, in_specs=in_specs, out_specs=out_specs, check_vma=False)
```

```python
import jax
import jax.numpy as jnp
from jax import lax
from jax.sharding import PartitionSpec as P

BLOCK = 64


adapter_scale = 0.5


def exchange_pieces(x, axis):
    count = lax.axis_size(axis)
    pieces = x.astype(jnp.bfloat16).reshape((count, x.shape[0] // count) + x.shape[1:])
    return lax.all_to_all(pieces, axis, 0, 0, tiled=False)


def scatter_sum(x, axis):
    return exchange_pieces(x, axis).astype(jnp.float32).sum(0)


def gather_rows(x, axis):
    count = lax.axis_size(axis)
    got = lax.all_to_all(jnp.broadcast_to(x[None], (count,) + x.shape), axis, 0, 0, tiled=False)
    return got.reshape((count * x.shape[0],) + x.shape[1:])


def shards(
    tokens,
    cotangent,
    gate_weight,
    up_weight,
    down_weight,
    gate_in,
    up_in,
    down_out,
    gate_out,
    up_out,
    down_in,
    tenants,
    owners,
):
    highest = lax.Precision.HIGHEST
    dp_count = lax.axis_size("dp")
    tensor_count = lax.axis_size("tensor")
    dp_index = lax.axis_index("dp")
    tensor_index = lax.axis_index("tensor")
    rows_in = tokens.shape[0]
    feat_here = tokens.shape[1]
    width_here = gate_weight.shape[1]
    rank_width = gate_in.shape[2]
    every_token_row = rows_in * tensor_count
    group_rows = every_token_row // dp_count
    blocks_all = tenants.shape[0]
    blocks_group = group_rows // BLOCK
    blocks_in = rows_in // BLOCK
    tenant_count = owners.shape[0]
    slots_here = tenant_count // dp_count
    tenants_here = tenant_count // tensor_count
    group_tenants = lax.dynamic_slice_in_dim(tenants, dp_index * blocks_group, blocks_group)
    input_tenants = lax.dynamic_slice_in_dim(tenants, tensor_index * blocks_in, blocks_in)
    contract_rows = (((0,), (0,)), ((), ()))
    token_tenants = jnp.broadcast_to(tenants[:, None], (blocks_all, BLOCK)).reshape(every_token_row)
    held_tenants = tensor_index * tenants_here + jnp.arange(tenants_here, dtype=jnp.int32)
    token_onehot = (token_tenants[:, None] == held_tenants[None, :]).astype(jnp.bfloat16)
    all_inputs = lax.all_gather(tokens, "tensor", axis=0, tiled=True)
    cotangent = lax.optimization_barrier((all_inputs, cotangent))[1]
    all_cot = lax.all_gather(cotangent, "tensor", axis=0, tiled=True)

    gate_part = jnp.dot(all_inputs, gate_weight, preferred_element_type=jnp.float32)
    up_part = jnp.dot(all_inputs, up_weight, preferred_element_type=jnp.float32)
    input_blocks = all_inputs.reshape(blocks_all, BLOCK, feat_here)
    gate_rank_part = jnp.einsum(
        "btk,bkr->btr", input_blocks, gate_in[tenants], preferred_element_type=jnp.float32
    ).reshape(every_token_row, rank_width)
    up_rank_part = jnp.einsum(
        "btk,bkr->btr", input_blocks, up_in[tenants], preferred_element_type=jnp.float32
    ).reshape(every_token_row, rank_width)
    forward_got = exchange_pieces(
        jnp.concatenate(
            [
                gate_part.astype(jnp.bfloat16),
                up_part.astype(jnp.bfloat16),
                gate_rank_part.astype(jnp.bfloat16),
                up_rank_part.astype(jnp.bfloat16),
            ],
            axis=1,
        ),
        "dp",
    )
    forward_sums = forward_got.astype(jnp.float32).sum(0)
    gate_total_sum = forward_sums[:, :width_here]
    up_total_sum = forward_sums[:, width_here : 2 * width_here]
    gate_rank = forward_sums[:, 2 * width_here : 2 * width_here + rank_width]
    up_rank = forward_sums[:, 2 * width_here + rank_width :]
    gate_rank_second = gate_rank.astype(jnp.bfloat16).reshape(blocks_group, BLOCK, rank_width)
    up_rank_second = up_rank.astype(jnp.bfloat16).reshape(blocks_group, BLOCK, rank_width)
    gate_raise = gate_out[group_tenants]
    up_raise = up_out[group_tenants]
    gate_complete = gate_total_sum + adapter_scale * jnp.einsum(
        "uim,umn->uin", gate_rank_second, gate_raise, preferred_element_type=jnp.float32
    ).reshape(group_rows, width_here)
    up_complete = up_total_sum + adapter_scale * jnp.einsum(
        "uim,umn->uin", up_rank_second, up_raise, preferred_element_type=jnp.float32
    ).reshape(group_rows, width_here)
    hidden = (jax.nn.silu(gate_complete) * up_complete).astype(jnp.bfloat16)
    all_hidden = gather_rows(hidden, "dp")

    hidden_grad_part = lax.dot_general(
        all_cot, down_weight, (((1,), (1,)), ((), ())), preferred_element_type=jnp.float32
    )
    down_back_part = adapter_scale * jnp.einsum(
        "env,ejv->enj",
        all_cot.reshape(blocks_all, BLOCK, feat_here),
        down_out[tenants],
        preferred_element_type=jnp.float32,
    ).reshape(every_token_row, rank_width)
    back_pieces = jnp.concatenate(
        [hidden_grad_part.astype(jnp.bfloat16), down_back_part.astype(jnp.bfloat16)], axis=1
    )
    forward_got, back_pieces = lax.optimization_barrier((forward_got, back_pieces))
    back_sums = scatter_sum(back_pieces, "dp")
    hidden_grad_sum = back_sums[:, :width_here]
    group_down_back = back_sums[:, width_here:].astype(jnp.bfloat16)
    down_drop = down_in[group_tenants]
    hidden_grad = hidden_grad_sum + jnp.einsum(
        "btr,bfr->btf",
        group_down_back.reshape(blocks_group, BLOCK, rank_width),
        down_drop,
        preferred_element_type=jnp.float32,
    ).reshape(group_rows, width_here)
    sig = jax.nn.sigmoid(gate_complete)
    up_gradient = (
        (hidden_grad * gate_complete * sig)
        .astype(jnp.bfloat16)
        .reshape(blocks_group, BLOCK, width_here)
    )
    gate_gradient = (
        (hidden_grad * up_complete * sig * (1.0 + gate_complete * (1.0 - sig)))
        .astype(jnp.bfloat16)
        .reshape(blocks_group, BLOCK, width_here)
    )
    gate_backward_piece = adapter_scale * jnp.einsum(
        "yae,yve->yav", gate_gradient, gate_raise, preferred_element_type=jnp.float32
    )
    up_backward_piece = adapter_scale * jnp.einsum(
        "yae,yve->yav", up_gradient, up_raise, preferred_element_type=jnp.float32
    )

    out_part = jnp.dot(all_hidden, down_weight, preferred_element_type=jnp.float32)
    down_rank_part = jnp.einsum(
        "btf,bfr->btr",
        all_hidden.reshape(blocks_all, BLOCK, width_here),
        down_in[tenants],
        preferred_element_type=jnp.float32,
    ).reshape(every_token_row, rank_width)
    rank_back_pieces = jnp.concatenate(
        [
            gate_backward_piece.reshape(group_rows, rank_width),
            up_backward_piece.reshape(group_rows, rank_width),
        ],
        axis=1,
    ).astype(jnp.bfloat16)
    down_pieces = jnp.concatenate(
        [out_part.astype(jnp.bfloat16), down_rank_part.astype(jnp.bfloat16)], axis=1
    ).reshape(tensor_count, rows_in, feat_here + rank_width)
    down_pieces = jnp.concatenate(
        [
            down_pieces,
            jnp.broadcast_to(rank_back_pieces[None], (tensor_count, group_rows, 2 * rank_width)),
        ],
        axis=2,
    )
    down_sums = scatter_sum(down_pieces.reshape(tensor_count * rows_in, -1), "tensor")
    out_sum = down_sums[:, :feat_here]
    down_rank_flat = down_sums[:, feat_here : feat_here + rank_width].astype(jnp.bfloat16)
    gate_backward = down_sums[:, feat_here + rank_width : feat_here + 2 * rank_width]
    up_backward = down_sums[:, feat_here + 2 * rank_width :]
    down_rank_second = down_rank_flat.reshape(blocks_in, BLOCK, rank_width)
    down_raise = down_out[input_tenants]
    mixed = (
        out_sum
        + adapter_scale
        * jnp.einsum(
            "vmn,vnx->vmx", down_rank_second, down_raise, preferred_element_type=jnp.float32
        ).reshape(rows_in, feat_here)
    ).astype(jnp.bfloat16)

    all_down_rank = gather_rows(down_rank_flat, "tensor")
    rank_weighted = (token_onehot[:, :, None] * all_down_rank[:, None, :]).reshape(
        every_token_row, tenants_here * rank_width
    )
    grad_down_out = adapter_scale * (
        lax.dot_general(rank_weighted, all_cot, contract_rows, preferred_element_type=jnp.float32)
        .reshape(tenants_here, rank_width, feat_here)
    )

    gate_raise_block_list = adapter_scale * jnp.einsum(
        "yap,yau->ypu", gate_rank_second, gate_gradient, preferred_element_type=jnp.float32
    )
    up_raise_block_list = adapter_scale * jnp.einsum(
        "yap,yau->ypu", up_rank_second, up_gradient, preferred_element_type=jnp.float32
    )
    raise_stack = jnp.stack([gate_raise_block_list, up_raise_block_list], axis=1).astype(
        jnp.bfloat16
    )
    backs = jnp.concatenate(
        [gate_backward.astype(jnp.bfloat16), up_backward.astype(jnp.bfloat16), group_down_back],
        axis=1,
    )
    raise_rows = raise_stack.reshape(-1, width_here)
    back_rows = -(-backs.size // (8 * width_here)) * 8
    backs_padded = jnp.pad(backs.reshape(-1), (0, back_rows * width_here - backs.size))
    all_joined = gather_rows(
        jnp.concatenate([raise_rows, backs_padded.reshape(back_rows, width_here)], axis=0), "dp"
    ).reshape(dp_count, -1, width_here)
    all_raise_blocks = (
        all_joined[:, : raise_rows.shape[0]]
        .reshape((dp_count * blocks_group,) + raise_stack.shape[1:])
        .astype(jnp.float32)
    )
    all_backs = (
        all_joined[:, raise_rows.shape[0] :]
        .reshape(dp_count, -1)[:, : backs.size]
        .reshape(every_token_row, 3 * rank_width)
    )
    own_slots = dp_index * slots_here + jnp.arange(slots_here, dtype=jnp.int32)
    block_onehot = (own_slots[:, None] == owners[tenants][None, :]).astype(jnp.float32)
    grad_gate_out = jnp.einsum(
        "sb,brf->srf", block_onehot, all_raise_blocks[:, 0], precision=highest
    )
    grad_up_out = jnp.einsum("sb,brf->srf", block_onehot, all_raise_blocks[:, 1], precision=highest)

    all_gate_back = all_backs[:, :rank_width]
    all_up_back = all_backs[:, rank_width : 2 * rank_width]
    all_down_back = all_backs[:, 2 * rank_width :]
    gate_weighted = (token_onehot[:, :, None] * all_gate_back[:, None, :]).reshape(
        every_token_row, tenants_here * rank_width
    )
    up_weighted = (token_onehot[:, :, None] * all_up_back[:, None, :]).reshape(
        every_token_row, tenants_here * rank_width
    )
    grad_gate_in = (
        lax.dot_general(
            all_inputs, gate_weighted, contract_rows, preferred_element_type=jnp.float32
        )
        .reshape(feat_here, tenants_here, rank_width)
        .transpose(1, 0, 2)
    )
    grad_up_in = (
        lax.dot_general(all_inputs, up_weighted, contract_rows, preferred_element_type=jnp.float32)
        .reshape(feat_here, tenants_here, rank_width)
        .transpose(1, 0, 2)
    )
    block_slot_onehot = (owners[tenants][:, None] == own_slots[None, :]).astype(jnp.bfloat16)
    slot_onehot = jnp.broadcast_to(
        block_slot_onehot[:, None, :], (blocks_all, BLOCK, slots_here)
    ).reshape(every_token_row, slots_here)
    drop_weighted = (slot_onehot[:, :, None] * all_down_back[:, None, :]).reshape(
        every_token_row, slots_here * rank_width
    )
    grad_down_in = (
        lax.dot_general(
            all_hidden, drop_weighted, contract_rows, preferred_element_type=jnp.float32
        )
        .reshape(width_here, slots_here, rank_width)
        .transpose(1, 0, 2)
    )
    return (
        mixed,
        grad_gate_in,
        grad_up_in,
        grad_down_out,
        grad_gate_out,
        grad_up_out,
        grad_down_in,
    )


def solution(mesh):
    in_specs = (
        P("tensor", "dp"),
        P("tensor", "dp"),
        P("dp", "tensor"),
        P("dp", "tensor"),
        P("tensor", "dp"),
        P(None, "dp", None),
        P(None, "dp", None),
        P(None, None, "dp"),
        P(None, None, "tensor"),
        P(None, None, "tensor"),
        P(None, "tensor", None),
        P(),
        P(),
    )
    out_specs = (
        P("tensor", "dp"),
        P("tensor", "dp", None),
        P("tensor", "dp", None),
        P("tensor", None, "dp"),
        P("dp", None, "tensor"),
        P("dp", None, "tensor"),
        P("dp", "tensor", None),
    )
    return jax.shard_map(shards, mesh=mesh, in_specs=in_specs, out_specs=out_specs, check_vma=False)
```

```python
import jax
import jax.numpy as jnp
from jax import lax
from jax.sharding import PartitionSpec as P

BLOCK = 64


adapter_scale = 0.5


def exchange_pieces(x, axis):
    count = lax.axis_size(axis)
    pieces = x.astype(jnp.bfloat16).reshape((count, x.shape[0] // count) + x.shape[1:])
    return lax.all_to_all(pieces, axis, 0, 0, tiled=False)


def scatter_sum(x, axis):
    return exchange_pieces(x, axis).astype(jnp.float32).sum(0)


def gather_rows(x, axis):
    count = lax.axis_size(axis)
    got = lax.all_to_all(jnp.broadcast_to(x[None], (count,) + x.shape), axis, 0, 0, tiled=False)
    return got.reshape((count * x.shape[0],) + x.shape[1:])


def shards(
    tokens,
    cotangent,
    gate_weight,
    up_weight,
    down_weight,
    gate_in,
    up_in,
    down_out,
    gate_out,
    up_out,
    down_in,
    tenants,
    owners,
):
    highest = lax.Precision.HIGHEST
    dp_count = lax.axis_size("dp")
    tensor_count = lax.axis_size("tensor")
    dp_index = lax.axis_index("dp")
    tensor_index = lax.axis_index("tensor")
    rows_in = tokens.shape[0]
    feat_here = tokens.shape[1]
    width_here = gate_weight.shape[1]
    rank_width = gate_in.shape[2]
    every_token_row = rows_in * tensor_count
    group_rows = every_token_row // dp_count
    blocks_all = tenants.shape[0]
    blocks_group = group_rows // BLOCK
    blocks_in = rows_in // BLOCK
    tenant_count = owners.shape[0]
    slots_here = tenant_count // dp_count
    tenants_here = tenant_count // tensor_count
    group_tenants = lax.dynamic_slice_in_dim(tenants, dp_index * blocks_group, blocks_group)
    input_tenants = lax.dynamic_slice_in_dim(tenants, tensor_index * blocks_in, blocks_in)
    contract_rows = (((0,), (0,)), ((), ()))
    token_tenants = jnp.broadcast_to(tenants[:, None], (blocks_all, BLOCK)).reshape(every_token_row)
    held_tenants = tensor_index * tenants_here + jnp.arange(tenants_here, dtype=jnp.int32)
    token_onehot = (token_tenants[:, None] == held_tenants[None, :]).astype(jnp.bfloat16)
    all_inputs = lax.all_gather(tokens, "tensor", axis=0, tiled=True)
    cotangent = lax.optimization_barrier((all_inputs, cotangent))[1]
    all_cot = lax.all_gather(cotangent, "tensor", axis=0, tiled=True)

    gate_part = jnp.dot(all_inputs, gate_weight, preferred_element_type=jnp.float32)
    up_part = jnp.dot(all_inputs, up_weight, preferred_element_type=jnp.float32)
    input_blocks = all_inputs.reshape(blocks_all, BLOCK, feat_here)
    gate_rank_part = jnp.einsum(
        "btk,bkr->btr", input_blocks, gate_in[tenants], preferred_element_type=jnp.float32
    ).reshape(every_token_row, rank_width)
    up_rank_part = jnp.einsum(
        "btk,bkr->btr", input_blocks, up_in[tenants], preferred_element_type=jnp.float32
    ).reshape(every_token_row, rank_width)
    gate_got = exchange_pieces(
        jnp.concatenate(
            [gate_part.astype(jnp.bfloat16), gate_rank_part.astype(jnp.bfloat16)], axis=1
        ),
        "dp",
    )
    up_got = exchange_pieces(
        jnp.concatenate([up_part.astype(jnp.bfloat16), up_rank_part.astype(jnp.bfloat16)], axis=1),
        "dp",
    )
    gate_sums = gate_got.astype(jnp.float32).sum(0)
    up_sums = up_got.astype(jnp.float32).sum(0)
    gate_total_sum = gate_sums[:, :width_here]
    up_total_sum = up_sums[:, :width_here]
    gate_rank = gate_sums[:, width_here:]
    up_rank = up_sums[:, width_here:]
    gate_rank_second = gate_rank.astype(jnp.bfloat16).reshape(blocks_group, BLOCK, rank_width)
    up_rank_second = up_rank.astype(jnp.bfloat16).reshape(blocks_group, BLOCK, rank_width)
    gate_raise = gate_out[group_tenants]
    up_raise = up_out[group_tenants]
    gate_complete = gate_total_sum + adapter_scale * jnp.einsum(
        "uim,umn->uin", gate_rank_second, gate_raise, preferred_element_type=jnp.float32
    ).reshape(group_rows, width_here)
    up_complete = up_total_sum + adapter_scale * jnp.einsum(
        "uim,umn->uin", up_rank_second, up_raise, preferred_element_type=jnp.float32
    ).reshape(group_rows, width_here)
    hidden = (jax.nn.silu(gate_complete) * up_complete).astype(jnp.bfloat16)
    all_hidden = gather_rows(hidden, "dp")

    hidden_grad_part = lax.dot_general(
        all_cot, down_weight, (((1,), (1,)), ((), ())), preferred_element_type=jnp.float32
    )
    down_back_part = adapter_scale * jnp.einsum(
        "env,ejv->enj",
        all_cot.reshape(blocks_all, BLOCK, feat_here),
        down_out[tenants],
        preferred_element_type=jnp.float32,
    ).reshape(every_token_row, rank_width)
    back_pieces = jnp.concatenate(
        [hidden_grad_part.astype(jnp.bfloat16), down_back_part.astype(jnp.bfloat16)], axis=1
    )
    gate_got, up_got, back_pieces = lax.optimization_barrier((gate_got, up_got, back_pieces))
    back_sums = scatter_sum(back_pieces, "dp")
    hidden_grad_sum = back_sums[:, :width_here]
    group_down_back = back_sums[:, width_here:].astype(jnp.bfloat16)
    down_drop = down_in[group_tenants]
    hidden_grad = hidden_grad_sum + jnp.einsum(
        "btr,bfr->btf",
        group_down_back.reshape(blocks_group, BLOCK, rank_width),
        down_drop,
        preferred_element_type=jnp.float32,
    ).reshape(group_rows, width_here)
    sig = jax.nn.sigmoid(gate_complete)
    up_gradient = (
        (hidden_grad * gate_complete * sig)
        .astype(jnp.bfloat16)
        .reshape(blocks_group, BLOCK, width_here)
    )
    gate_gradient = (
        (hidden_grad * up_complete * sig * (1.0 + gate_complete * (1.0 - sig)))
        .astype(jnp.bfloat16)
        .reshape(blocks_group, BLOCK, width_here)
    )
    gate_backward_piece = adapter_scale * jnp.einsum(
        "yae,yve->yav", gate_gradient, gate_raise, preferred_element_type=jnp.float32
    )
    up_backward_piece = adapter_scale * jnp.einsum(
        "yae,yve->yav", up_gradient, up_raise, preferred_element_type=jnp.float32
    )

    out_part = jnp.dot(all_hidden, down_weight, preferred_element_type=jnp.float32)
    down_rank_part = jnp.einsum(
        "btf,bfr->btr",
        all_hidden.reshape(blocks_all, BLOCK, width_here),
        down_in[tenants],
        preferred_element_type=jnp.float32,
    ).reshape(every_token_row, rank_width)
    rank_back_pieces = jnp.concatenate(
        [
            gate_backward_piece.reshape(group_rows, rank_width),
            up_backward_piece.reshape(group_rows, rank_width),
        ],
        axis=1,
    ).astype(jnp.bfloat16)
    down_pieces = jnp.concatenate(
        [out_part.astype(jnp.bfloat16), down_rank_part.astype(jnp.bfloat16)], axis=1
    ).reshape(tensor_count, rows_in, feat_here + rank_width)
    down_pieces = jnp.concatenate(
        [
            down_pieces,
            jnp.broadcast_to(rank_back_pieces[None], (tensor_count, group_rows, 2 * rank_width)),
        ],
        axis=2,
    )
    down_sums = scatter_sum(down_pieces.reshape(tensor_count * rows_in, -1), "tensor")
    out_sum = down_sums[:, :feat_here]
    down_rank_flat = down_sums[:, feat_here : feat_here + rank_width].astype(jnp.bfloat16)
    gate_backward = down_sums[:, feat_here + rank_width : feat_here + 2 * rank_width]
    up_backward = down_sums[:, feat_here + 2 * rank_width :]
    down_rank_second = down_rank_flat.reshape(blocks_in, BLOCK, rank_width)
    down_raise = down_out[input_tenants]
    mixed = (
        out_sum
        + adapter_scale
        * jnp.einsum(
            "vmn,vnx->vmx", down_rank_second, down_raise, preferred_element_type=jnp.float32
        ).reshape(rows_in, feat_here)
    ).astype(jnp.bfloat16)

    all_down_rank = lax.all_gather(down_rank_flat, "tensor", axis=0, tiled=True)
    rank_weighted = (token_onehot[:, :, None] * all_down_rank[:, None, :]).reshape(
        every_token_row, tenants_here * rank_width
    )
    grad_down_out = adapter_scale * (
        lax.dot_general(rank_weighted, all_cot, contract_rows, preferred_element_type=jnp.float32)
        .reshape(tenants_here, rank_width, feat_here)
    )

    gate_raise_block_list = adapter_scale * jnp.einsum(
        "yap,yau->ypu", gate_rank_second, gate_gradient, preferred_element_type=jnp.float32
    )
    up_raise_block_list = adapter_scale * jnp.einsum(
        "yap,yau->ypu", up_rank_second, up_gradient, preferred_element_type=jnp.float32
    )
    raise_stack = jnp.stack([gate_raise_block_list, up_raise_block_list], axis=1).astype(
        jnp.bfloat16
    )
    backs = jnp.concatenate(
        [gate_backward.astype(jnp.bfloat16), up_backward.astype(jnp.bfloat16), group_down_back],
        axis=1,
    )
    raise_rows = raise_stack.reshape(-1, width_here)
    back_rows = -(-backs.size // (8 * width_here)) * 8
    backs_padded = jnp.pad(backs.reshape(-1), (0, back_rows * width_here - backs.size))
    all_joined = gather_rows(
        jnp.concatenate([raise_rows, backs_padded.reshape(back_rows, width_here)], axis=0), "dp"
    ).reshape(dp_count, -1, width_here)
    all_raise_blocks = (
        all_joined[:, : raise_rows.shape[0]]
        .reshape((dp_count * blocks_group,) + raise_stack.shape[1:])
        .astype(jnp.float32)
    )
    all_backs = (
        all_joined[:, raise_rows.shape[0] :]
        .reshape(dp_count, -1)[:, : backs.size]
        .reshape(every_token_row, 3 * rank_width)
    )
    own_slots = dp_index * slots_here + jnp.arange(slots_here, dtype=jnp.int32)
    block_onehot = (own_slots[:, None] == owners[tenants][None, :]).astype(jnp.float32)
    grad_gate_out = jnp.einsum(
        "sb,brf->srf", block_onehot, all_raise_blocks[:, 0], precision=highest
    )
    grad_up_out = jnp.einsum("sb,brf->srf", block_onehot, all_raise_blocks[:, 1], precision=highest)

    all_gate_back = all_backs[:, :rank_width]
    all_up_back = all_backs[:, rank_width : 2 * rank_width]
    all_down_back = all_backs[:, 2 * rank_width :]
    gate_weighted = (token_onehot[:, :, None] * all_gate_back[:, None, :]).reshape(
        every_token_row, tenants_here * rank_width
    )
    up_weighted = (token_onehot[:, :, None] * all_up_back[:, None, :]).reshape(
        every_token_row, tenants_here * rank_width
    )
    grad_gate_in = (
        lax.dot_general(
            all_inputs, gate_weighted, contract_rows, preferred_element_type=jnp.float32
        )
        .reshape(feat_here, tenants_here, rank_width)
        .transpose(1, 0, 2)
    )
    grad_up_in = (
        lax.dot_general(all_inputs, up_weighted, contract_rows, preferred_element_type=jnp.float32)
        .reshape(feat_here, tenants_here, rank_width)
        .transpose(1, 0, 2)
    )
    block_slot_onehot = (owners[tenants][:, None] == own_slots[None, :]).astype(jnp.bfloat16)
    slot_onehot = jnp.broadcast_to(
        block_slot_onehot[:, None, :], (blocks_all, BLOCK, slots_here)
    ).reshape(every_token_row, slots_here)
    drop_weighted = (slot_onehot[:, :, None] * all_down_back[:, None, :]).reshape(
        every_token_row, slots_here * rank_width
    )
    grad_down_in = (
        lax.dot_general(
            all_hidden, drop_weighted, contract_rows, preferred_element_type=jnp.float32
        )
        .reshape(width_here, slots_here, rank_width)
        .transpose(1, 0, 2)
    )
    return (
        mixed,
        grad_gate_in,
        grad_up_in,
        grad_down_out,
        grad_gate_out,
        grad_up_out,
        grad_down_in,
    )


def solution(mesh):
    in_specs = (
        P("tensor", "dp"),
        P("tensor", "dp"),
        P("dp", "tensor"),
        P("dp", "tensor"),
        P("tensor", "dp"),
        P(None, "dp", None),
        P(None, "dp", None),
        P(None, None, "dp"),
        P(None, None, "tensor"),
        P(None, None, "tensor"),
        P(None, "tensor", None),
        P(),
        P(),
    )
    out_specs = (
        P("tensor", "dp"),
        P("tensor", "dp", None),
        P("tensor", "dp", None),
        P("tensor", None, "dp"),
        P("dp", None, "tensor"),
        P("dp", None, "tensor"),
        P("dp", "tensor", None),
    )
    return jax.shard_map(shards, mesh=mesh, in_specs=in_specs, out_specs=out_specs, check_vma=False)
```

```python
import jax
import jax.numpy as jnp
from jax import lax
from jax.sharding import PartitionSpec as P

BLOCK = 64


adapter_scale = 0.5


def exchange_pieces(x, axis):
    count = lax.axis_size(axis)
    pieces = x.astype(jnp.bfloat16).reshape((count, x.shape[0] // count) + x.shape[1:])
    return lax.all_to_all(pieces, axis, 0, 0, tiled=False)


def scatter_sum(x, axis):
    return exchange_pieces(x, axis).astype(jnp.float32).sum(0)


def gather_rows(x, axis):
    count = lax.axis_size(axis)
    got = lax.all_to_all(jnp.broadcast_to(x[None], (count,) + x.shape), axis, 0, 0, tiled=False)
    return got.reshape((count * x.shape[0],) + x.shape[1:])


def shards(
    tokens,
    cotangent,
    gate_weight,
    up_weight,
    down_weight,
    gate_in,
    up_in,
    down_out,
    gate_out,
    up_out,
    down_in,
    tenants,
    owners,
):
    highest = lax.Precision.HIGHEST
    dp_count = lax.axis_size("dp")
    tensor_count = lax.axis_size("tensor")
    dp_index = lax.axis_index("dp")
    tensor_index = lax.axis_index("tensor")
    rows_in = tokens.shape[0]
    feat_here = tokens.shape[1]
    width_here = gate_weight.shape[1]
    rank_width = gate_in.shape[2]
    every_token_row = rows_in * tensor_count
    group_rows = every_token_row // dp_count
    blocks_all = tenants.shape[0]
    blocks_group = group_rows // BLOCK
    blocks_in = rows_in // BLOCK
    tenant_count = owners.shape[0]
    slots_here = tenant_count // dp_count
    tenants_here = tenant_count // tensor_count
    group_tenants = lax.dynamic_slice_in_dim(tenants, dp_index * blocks_group, blocks_group)
    input_tenants = lax.dynamic_slice_in_dim(tenants, tensor_index * blocks_in, blocks_in)
    contract_rows = (((0,), (0,)), ((), ()))
    token_tenants = jnp.broadcast_to(tenants[:, None], (blocks_all, BLOCK)).reshape(every_token_row)
    held_tenants = tensor_index * tenants_here + jnp.arange(tenants_here, dtype=jnp.int32)
    token_onehot = (token_tenants[:, None] == held_tenants[None, :]).astype(jnp.bfloat16)
    all_inputs = lax.all_gather(tokens, "tensor", axis=0, tiled=True)
    cotangent = lax.optimization_barrier((all_inputs, cotangent))[1]
    all_cot = lax.all_gather(cotangent, "tensor", axis=0, tiled=True)

    gate_part = jnp.dot(all_inputs, gate_weight, preferred_element_type=jnp.float32)
    up_part = jnp.dot(all_inputs, up_weight, preferred_element_type=jnp.float32)
    input_blocks = all_inputs.reshape(blocks_all, BLOCK, feat_here)
    gate_rank_part = jnp.einsum(
        "btk,bkr->btr", input_blocks, gate_in[tenants], preferred_element_type=jnp.float32
    ).reshape(every_token_row, rank_width)
    up_rank_part = jnp.einsum(
        "btk,bkr->btr", input_blocks, up_in[tenants], preferred_element_type=jnp.float32
    ).reshape(every_token_row, rank_width)
    cut = width_here // 7 * 4
    gate_head = exchange_pieces(gate_part[:, :cut], "dp")
    gate_got = exchange_pieces(
        jnp.concatenate(
            [gate_part[:, cut:].astype(jnp.bfloat16), gate_rank_part.astype(jnp.bfloat16)], axis=1
        ),
        "dp",
    )
    up_head = exchange_pieces(up_part[:, :cut], "dp")
    up_got = exchange_pieces(
        jnp.concatenate(
            [up_part[:, cut:].astype(jnp.bfloat16), up_rank_part.astype(jnp.bfloat16)], axis=1
        ),
        "dp",
    )
    gate_got = jnp.concatenate([gate_head, gate_got], axis=2)
    up_got = jnp.concatenate([up_head, up_got], axis=2)
    gate_sums = gate_got.astype(jnp.float32).sum(0)
    up_sums = up_got.astype(jnp.float32).sum(0)
    gate_total_sum = gate_sums[:, :width_here]
    up_total_sum = up_sums[:, :width_here]
    gate_rank = gate_sums[:, width_here:]
    up_rank = up_sums[:, width_here:]
    gate_rank_second = gate_rank.astype(jnp.bfloat16).reshape(blocks_group, BLOCK, rank_width)
    up_rank_second = up_rank.astype(jnp.bfloat16).reshape(blocks_group, BLOCK, rank_width)
    gate_raise = gate_out[group_tenants]
    up_raise = up_out[group_tenants]
    gate_complete = gate_total_sum + adapter_scale * jnp.einsum(
        "uim,umn->uin", gate_rank_second, gate_raise, preferred_element_type=jnp.float32
    ).reshape(group_rows, width_here)
    up_complete = up_total_sum + adapter_scale * jnp.einsum(
        "uim,umn->uin", up_rank_second, up_raise, preferred_element_type=jnp.float32
    ).reshape(group_rows, width_here)
    hidden = (jax.nn.silu(gate_complete) * up_complete).astype(jnp.bfloat16)
    all_hidden = gather_rows(hidden, "dp")

    hidden_grad_part = lax.dot_general(
        all_cot, down_weight, (((1,), (1,)), ((), ())), preferred_element_type=jnp.float32
    )
    down_back_part = adapter_scale * jnp.einsum(
        "env,ejv->enj",
        all_cot.reshape(blocks_all, BLOCK, feat_here),
        down_out[tenants],
        preferred_element_type=jnp.float32,
    ).reshape(every_token_row, rank_width)
    back_pieces = jnp.concatenate(
        [hidden_grad_part.astype(jnp.bfloat16), down_back_part.astype(jnp.bfloat16)], axis=1
    )
    gate_got, up_got, back_pieces = lax.optimization_barrier((gate_got, up_got, back_pieces))
    back_sums = scatter_sum(back_pieces, "dp")
    hidden_grad_sum = back_sums[:, :width_here]
    group_down_back = back_sums[:, width_here:].astype(jnp.bfloat16)
    down_drop = down_in[group_tenants]
    hidden_grad = hidden_grad_sum + jnp.einsum(
        "btr,bfr->btf",
        group_down_back.reshape(blocks_group, BLOCK, rank_width),
        down_drop,
        preferred_element_type=jnp.float32,
    ).reshape(group_rows, width_here)
    sig = jax.nn.sigmoid(gate_complete)
    up_gradient = (
        (hidden_grad * gate_complete * sig)
        .astype(jnp.bfloat16)
        .reshape(blocks_group, BLOCK, width_here)
    )
    gate_gradient = (
        (hidden_grad * up_complete * sig * (1.0 + gate_complete * (1.0 - sig)))
        .astype(jnp.bfloat16)
        .reshape(blocks_group, BLOCK, width_here)
    )
    gate_backward_piece = adapter_scale * jnp.einsum(
        "yae,yve->yav", gate_gradient, gate_raise, preferred_element_type=jnp.float32
    )
    up_backward_piece = adapter_scale * jnp.einsum(
        "yae,yve->yav", up_gradient, up_raise, preferred_element_type=jnp.float32
    )

    out_part = jnp.dot(all_hidden, down_weight, preferred_element_type=jnp.float32)
    down_rank_part = jnp.einsum(
        "btf,bfr->btr",
        all_hidden.reshape(blocks_all, BLOCK, width_here),
        down_in[tenants],
        preferred_element_type=jnp.float32,
    ).reshape(every_token_row, rank_width)
    rank_back_pieces = jnp.concatenate(
        [
            gate_backward_piece.reshape(group_rows, rank_width),
            up_backward_piece.reshape(group_rows, rank_width),
        ],
        axis=1,
    ).astype(jnp.bfloat16)
    down_pieces = jnp.concatenate(
        [out_part.astype(jnp.bfloat16), down_rank_part.astype(jnp.bfloat16)], axis=1
    ).reshape(tensor_count, rows_in, feat_here + rank_width)
    down_pieces = jnp.concatenate(
        [
            down_pieces,
            jnp.broadcast_to(rank_back_pieces[None], (tensor_count, group_rows, 2 * rank_width)),
        ],
        axis=2,
    )
    down_sums = scatter_sum(down_pieces.reshape(tensor_count * rows_in, -1), "tensor")
    out_sum = down_sums[:, :feat_here]
    down_rank_flat = down_sums[:, feat_here : feat_here + rank_width].astype(jnp.bfloat16)
    gate_backward = down_sums[:, feat_here + rank_width : feat_here + 2 * rank_width]
    up_backward = down_sums[:, feat_here + 2 * rank_width :]
    down_rank_second = down_rank_flat.reshape(blocks_in, BLOCK, rank_width)
    down_raise = down_out[input_tenants]
    mixed = (
        out_sum
        + adapter_scale
        * jnp.einsum(
            "vmn,vnx->vmx", down_rank_second, down_raise, preferred_element_type=jnp.float32
        ).reshape(rows_in, feat_here)
    ).astype(jnp.bfloat16)

    all_down_rank = lax.all_gather(down_rank_flat, "tensor", axis=0, tiled=True)
    rank_weighted = (token_onehot[:, :, None] * all_down_rank[:, None, :]).reshape(
        every_token_row, tenants_here * rank_width
    )
    grad_down_out = adapter_scale * (
        lax.dot_general(rank_weighted, all_cot, contract_rows, preferred_element_type=jnp.float32)
        .reshape(tenants_here, rank_width, feat_here)
    )

    gate_raise_block_list = adapter_scale * jnp.einsum(
        "yap,yau->ypu", gate_rank_second, gate_gradient, preferred_element_type=jnp.float32
    )
    up_raise_block_list = adapter_scale * jnp.einsum(
        "yap,yau->ypu", up_rank_second, up_gradient, preferred_element_type=jnp.float32
    )
    raise_stack = jnp.stack([gate_raise_block_list, up_raise_block_list], axis=1).astype(
        jnp.bfloat16
    )
    backs = jnp.concatenate(
        [gate_backward.astype(jnp.bfloat16), up_backward.astype(jnp.bfloat16), group_down_back],
        axis=1,
    )
    raise_rows = raise_stack.reshape(-1, width_here)
    back_rows = -(-backs.size // (8 * width_here)) * 8
    backs_padded = jnp.pad(backs.reshape(-1), (0, back_rows * width_here - backs.size))
    all_joined = gather_rows(
        jnp.concatenate([raise_rows, backs_padded.reshape(back_rows, width_here)], axis=0), "dp"
    ).reshape(dp_count, -1, width_here)
    all_raise_blocks = (
        all_joined[:, : raise_rows.shape[0]]
        .reshape((dp_count * blocks_group,) + raise_stack.shape[1:])
        .astype(jnp.float32)
    )
    all_backs = (
        all_joined[:, raise_rows.shape[0] :]
        .reshape(dp_count, -1)[:, : backs.size]
        .reshape(every_token_row, 3 * rank_width)
    )
    own_slots = dp_index * slots_here + jnp.arange(slots_here, dtype=jnp.int32)
    block_onehot = (own_slots[:, None] == owners[tenants][None, :]).astype(jnp.float32)
    grad_gate_out = jnp.einsum(
        "sb,brf->srf", block_onehot, all_raise_blocks[:, 0], precision=highest
    )
    grad_up_out = jnp.einsum("sb,brf->srf", block_onehot, all_raise_blocks[:, 1], precision=highest)

    all_gate_back = all_backs[:, :rank_width]
    all_up_back = all_backs[:, rank_width : 2 * rank_width]
    all_down_back = all_backs[:, 2 * rank_width :]
    gate_weighted = (token_onehot[:, :, None] * all_gate_back[:, None, :]).reshape(
        every_token_row, tenants_here * rank_width
    )
    up_weighted = (token_onehot[:, :, None] * all_up_back[:, None, :]).reshape(
        every_token_row, tenants_here * rank_width
    )
    grad_gate_in = (
        lax.dot_general(
            all_inputs, gate_weighted, contract_rows, preferred_element_type=jnp.float32
        )
        .reshape(feat_here, tenants_here, rank_width)
        .transpose(1, 0, 2)
    )
    grad_up_in = (
        lax.dot_general(all_inputs, up_weighted, contract_rows, preferred_element_type=jnp.float32)
        .reshape(feat_here, tenants_here, rank_width)
        .transpose(1, 0, 2)
    )
    block_slot_onehot = (owners[tenants][:, None] == own_slots[None, :]).astype(jnp.bfloat16)
    slot_onehot = jnp.broadcast_to(
        block_slot_onehot[:, None, :], (blocks_all, BLOCK, slots_here)
    ).reshape(every_token_row, slots_here)
    drop_weighted = (slot_onehot[:, :, None] * all_down_back[:, None, :]).reshape(
        every_token_row, slots_here * rank_width
    )
    grad_down_in = (
        lax.dot_general(
            all_hidden, drop_weighted, contract_rows, preferred_element_type=jnp.float32
        )
        .reshape(width_here, slots_here, rank_width)
        .transpose(1, 0, 2)
    )
    return (
        mixed,
        grad_gate_in,
        grad_up_in,
        grad_down_out,
        grad_gate_out,
        grad_up_out,
        grad_down_in,
    )


def solution(mesh):
    in_specs = (
        P("tensor", "dp"),
        P("tensor", "dp"),
        P("dp", "tensor"),
        P("dp", "tensor"),
        P("tensor", "dp"),
        P(None, "dp", None),
        P(None, "dp", None),
        P(None, None, "dp"),
        P(None, None, "tensor"),
        P(None, None, "tensor"),
        P(None, "tensor", None),
        P(),
        P(),
    )
    out_specs = (
        P("tensor", "dp"),
        P("tensor", "dp", None),
        P("tensor", "dp", None),
        P("tensor", None, "dp"),
        P("dp", None, "tensor"),
        P("dp", None, "tensor"),
        P("dp", "tensor", None),
    )
    return jax.shard_map(shards, mesh=mesh, in_specs=in_specs, out_specs=out_specs, check_vma=False)
```
